32 devices in a mesh: groups: 2 (over x), ctx: 8 (over z, y), head: 2 (over core).
Axes of the slice: x: 2, y: 2, z: 4, core: 2. Of those that a mesh axis runs over, the one named last changes fastest.
Arguments:
- query_matrix: bfloat16 [6144, 4096], P(('groups', 'ctx', 'head')), parts along dimension 0, may hold values from -6 to 6
- key_matrix: bfloat16 [6144, 1024], P(('groups', 'ctx', 'head')), parts along dimension 0, may hold values from -6 to 6
- value_matrix: bfloat16 [6144, 1024], P(('groups', 'ctx', 'head')), parts along dimension 0, may hold values from -6 to 6
- fwd_output: bfloat16 [6144, 4096], P(('groups', 'ctx', 'head')), parts along dimension 0, may hold values from -6 to 6
- output_gradient: bfloat16 [6144, 4096], P(('groups', 'ctx', 'head')), parts along dimension 0, may hold values from -6 to 6
- block_docs: int32 [48], P('groups'), parts along dimension 0, may hold values from 0 to 11, never falling along the last dimension, each value on 1 to 6 neighbouring positions
Outputs:
- query_grad: bfloat16 [6144, 4096], P(('groups', 'ctx', 'head')), parts along dimension 0
- key_grad: bfloat16 [6144, 1024], P(('groups', 'ctx', 'head')), parts along dimension 0
- value_grad: bfloat16 [6144, 1024], P(('groups', 'ctx', 'head')), parts along dimension 0
The draws below stay inside these ranges and needn't reach their ends.
There are 2 independent parts, one for each index of `groups`. The reference program is written for one: setup_inputs(seed, part) draws one part's arguments, and reference() takes and returns one part's arrays. A program takes and returns all parts, laid end to end along the dimension named above; each array names one. Nothing has to cross between parts.
Inputs may be any that keep to these rules, and one draw needn't show every extreme that they name: `block_docs`: never falls along the sequence; every document covers 1 to 6 blocks, and one covers exactly 6.
All inputs are finite; a program needn't handle non-finite values.
Results may differ from the reference program's by a relative error of at most 0.005.
Values may be sent and summed in bfloat16 or wider, within the bound.
No kernel may reach another device: no remote copies, remote signals or barrier semaphores. Data moves between devices by JAX's collectives and lax.ppermute only.
A program may use at most 128 MiB of HBM per device.

```python
import math
import jax
import jax.numpy as jnp
import numpy as np
from jax import lax

QUERY_HEADS = 32
KEY_VALUE_HEADS = 8
HEAD_SIZE = 128
BLK = 128
CB = 3
REACH = 2
PACKED_TOKENS = 3072
NBLK = 24
DOCS = 12
DOC_MOST = 6


def paired_draw(key):
    query_group = QUERY_HEADS // KEY_VALUE_HEADS
    random_query_seed = jax.random.fold_in(key, 101)
    random_key_seed = jax.random.fold_in(key, 102)
    every_query_row = jnp.clip(jax.random.normal(random_query_seed, (PACKED_TOKENS, KEY_VALUE_HEADS, query_group, HEAD_SIZE), jnp.float32), -6.0, 6.0)
    every_key_row = jnp.clip(jax.random.normal(random_key_seed, (PACKED_TOKENS, KEY_VALUE_HEADS, HEAD_SIZE), jnp.float32), -6.0, 6.0)
    return (every_query_row.reshape(PACKED_TOKENS, QUERY_HEADS * HEAD_SIZE).astype(jnp.bfloat16), every_key_row.reshape(PACKED_TOKENS, KEY_VALUE_HEADS * HEAD_SIZE).astype(jnp.bfloat16))


def draw_query_matrix(key, part):
    return paired_draw(key)[0]


def draw_key_matrix(key, part):
    return paired_draw(key)[1]


def block_scale(key, shape, cuts, least, high):
    level, own = 1.0, jax.random.fold_in(key, 6)
    for dim, blocks in cuts:
        steps = jnp.exp(jax.random.uniform(jax.random.fold_in(own, dim), (blocks,), jnp.float32, least / len(cuts), high / len(cuts)))
        level = level * jnp.repeat(steps, shape[dim] // blocks).reshape([-1 if axis == dim else 1 for axis in range(len(shape))])
    return level


def split_up(number_of, total, bound, skew):
    loads = [(1 << 20) // math.isqrt(rank ** skew) + 1 for rank in range(2, number_of + 1)]
    surplus, given = total - bound - (number_of - 1), [1] * (number_of - 1)
    while surplus > 0:
        candidates = [i for i in range(number_of - 1) if given[i] < bound]
        pool, remaining = sum([loads[i] for i in candidates]), surplus
        for i in candidates:
            addition = min(bound - given[i], max(1, remaining * loads[i] // pool), surplus)
            given[i] = given[i] + addition
            surplus = surplus - addition
    return np.array([bound] + given)


def uneven(rng, amount, total, bound, skew):
    if amount == 2:
        one = jax.random.randint(rng, (), max(1, total - bound), min(bound, total - 1) + 1)
        return jnp.stack([one, total - one])
    tallies = jnp.asarray(split_up(amount, total, bound, skew), jnp.int32)
    twos = (amount - 1) // 2
    donor, receiver = tallies[1:1 + 2 * twos:2], tallies[2:2 + 2 * twos:2]
    margin = jnp.minimum(donor - 1, bound - receiver)
    shifted = jax.random.randint(jax.random.fold_in(rng, 1), (twos,), 0, 1 << 20) % (margin + 1)
    tallies = tallies.at[1:1 + 2 * twos:2].set(donor - shifted).at[2:2 + 2 * twos:2].set(receiver + shifted)
    return tallies[jax.random.permutation(jax.random.fold_in(rng, 2), amount)]


def gaussian(own_key, dims, width, limit, cuts=(), kind=jnp.bfloat16):
    values = jax.random.normal(own_key, dims, jnp.float32) * width
    if len(cuts) > 0:
        values = block_scale(own_key, dims, cuts, -0.22, 0.18) * values
    return jnp.clip(values, min=-limit, max=limit).astype(kind)


def setup_inputs(seed: int = 0, part: int = 0) -> dict:
    streams_of = jax.random.split(jax.random.key(seed), 7)
    own_keys = jax.random.split(jax.random.fold_in(streams_of[6], part), 7)
    return {
        "query_matrix": draw_query_matrix(jax.random.fold_in(jax.random.fold_in(streams_of[6], part), 71), part),
        "key_matrix": draw_key_matrix(jax.random.fold_in(jax.random.fold_in(streams_of[6], part), 71), part),
        "value_matrix": gaussian(own_keys[2], (PACKED_TOKENS, KEY_VALUE_HEADS * HEAD_SIZE), 1.0, 6.0, ((0, 16),)),
        "fwd_output": gaussian(own_keys[3], (PACKED_TOKENS, QUERY_HEADS * HEAD_SIZE), 1.0, 6.0, ((0, 16),)),
        "output_gradient": gaussian(own_keys[4], (PACKED_TOKENS, QUERY_HEADS * HEAD_SIZE), 1.0, 6.0, ((0, 16),)),
        "block_docs": jnp.searchsorted(jnp.cumsum(uneven(own_keys[5], DOCS, NBLK, DOC_MOST, 2)), jnp.arange(NBLK), side="right").astype(jnp.int32),
    }


def reference(query_matrix, key_matrix, value_matrix, fwd_output, output_gradient, block_docs):
    query_group = QUERY_HEADS // KEY_VALUE_HEADS
    window_extent = CB * BLK
    padding_extent = REACH * window_extent
    scale = HEAD_SIZE ** -0.5
    nblocks = PACKED_TOKENS // window_extent
    token_docs = jnp.repeat(block_docs.astype(jnp.int32), BLK)
    pad_docs = jnp.concatenate([jnp.full((padding_extent,), -1, jnp.int32), token_docs])
    padded_keys = jnp.concatenate([jnp.zeros((padding_extent, KEY_VALUE_HEADS * HEAD_SIZE), key_matrix.dtype), key_matrix])
    padded_values = jnp.concatenate([jnp.zeros((padding_extent, KEY_VALUE_HEADS * HEAD_SIZE), value_matrix.dtype), value_matrix])
    output_dot_gradient = jnp.sum(output_gradient.astype(jnp.float32).reshape(PACKED_TOKENS, QUERY_HEADS, HEAD_SIZE)
                    * fwd_output.astype(jnp.float32).reshape(PACKED_TOKENS, QUERY_HEADS, HEAD_SIZE), axis=2)

    def step(carry, index):
        key_gradient_total, value_gradient_total = carry
        window_begin = (index * window_extent).astype(jnp.int32)
        query_block = lax.dynamic_slice_in_dim(query_matrix, window_begin, window_extent, 0).astype(jnp.float32).reshape(window_extent, KEY_VALUE_HEADS, query_group, HEAD_SIZE)
        gradient_block = lax.dynamic_slice_in_dim(output_gradient, window_begin, window_extent, 0).astype(jnp.float32).reshape(window_extent, KEY_VALUE_HEADS, query_group, HEAD_SIZE)
        document_block = lax.dynamic_slice_in_dim(output_dot_gradient, window_begin, window_extent, 0).reshape(window_extent, KEY_VALUE_HEADS, query_group)
        document_block = jnp.transpose(document_block, (1, 2, 0))[..., None]
        key_window = lax.dynamic_slice_in_dim(padded_keys, window_begin, padding_extent + window_extent, 0).astype(jnp.float32).reshape(padding_extent + window_extent, KEY_VALUE_HEADS, HEAD_SIZE)
        value_window = lax.dynamic_slice_in_dim(padded_values, window_begin, padding_extent + window_extent, 0).astype(jnp.float32).reshape(padding_extent + window_extent, KEY_VALUE_HEADS, HEAD_SIZE)
        qdoc = lax.dynamic_slice_in_dim(token_docs, window_begin, window_extent, 0)
        kdoc = lax.dynamic_slice_in_dim(pad_docs, window_begin, padding_extent + window_extent, 0)
        qpos = window_begin + jnp.arange(window_extent, dtype=jnp.int32)
        kpos = window_begin - padding_extent + jnp.arange(padding_extent + window_extent, dtype=jnp.int32)
        mask = (qdoc[:, None] == kdoc[None, :]) & (kpos[None, :] <= qpos[:, None])
        scores = scale * jnp.einsum('qgrd,kgd->grqk', query_block, key_window)
        masked = jnp.where(mask, scores, -1e30)
        top = jnp.max(masked, axis=3, keepdims=True)
        total = jnp.sum(jnp.where(mask, jnp.exp(masked - top), 0.0), axis=3, keepdims=True)
        lse = top + jnp.log(total)
        probs = jnp.where(mask, jnp.exp(masked - lse), 0.0)
        probs_low = probs.astype(jnp.bfloat16)
        dprob = jnp.einsum('qgrd,kgd->grqk', gradient_block, value_window)
        dscore = (probs * (dprob - document_block)).astype(jnp.bfloat16).astype(jnp.float32)
        part_q = scale * jnp.einsum('grqk,kgd->qgrd', dscore, key_window)
        partial_key_gradient = scale * jnp.einsum('grqk,qgrd->kgd', dscore, query_block)
        partial_value_gradient = jnp.einsum('grqk,qgrd->kgd', probs_low.astype(jnp.float32), gradient_block)
        previous_key = lax.dynamic_slice_in_dim(key_gradient_total, window_begin, padding_extent + window_extent, 0)
        previous_value = lax.dynamic_slice_in_dim(value_gradient_total, window_begin, padding_extent + window_extent, 0)
        key_gradient_total = lax.dynamic_update_slice_in_dim(key_gradient_total, previous_key + partial_key_gradient.reshape(padding_extent + window_extent, KEY_VALUE_HEADS * HEAD_SIZE), window_begin, 0)
        value_gradient_total = lax.dynamic_update_slice_in_dim(value_gradient_total, previous_value + partial_value_gradient.reshape(padding_extent + window_extent, KEY_VALUE_HEADS * HEAD_SIZE), window_begin, 0)
        return (key_gradient_total, value_gradient_total), part_q.reshape(window_extent, QUERY_HEADS * HEAD_SIZE).astype(jnp.bfloat16)

    zero_filled = jnp.zeros((padding_extent + PACKED_TOKENS, KEY_VALUE_HEADS * HEAD_SIZE), jnp.float32)
    (key_gradient_total, value_gradient_total), query_parts = lax.scan(step, (zero_filled, zero_filled), jnp.arange(nblocks, dtype=jnp.int32))
    query_grad = query_parts.reshape(PACKED_TOKENS, QUERY_HEADS * HEAD_SIZE)
    return query_grad, key_gradient_total[padding_extent:].astype(jnp.bfloat16), value_gradient_total[padding_extent:].astype(jnp.bfloat16)
```

```python
import functools

import jax
import jax.numpy as jnp
from jax import lax
from jax.experimental import pallas as pl
from jax.experimental.pallas import tpu as pltpu
from jax.sharding import PartitionSpec as P

HEAD_SIZE = 128
BLK = 128
REACH = 2
DOC_MOST = 6


def shifted(block, axis, distance):
    devices = range(lax.axis_size(axis))
    route = [(i - distance, i) for i in devices if i - distance in devices]
    return lax.ppermute(block, axis, route)


def attention_kernel(qdoc_ref, kdoc_ref, q_ref, do_ref, o_ref, k_ref, v_ref,
                     dq_ref, dk_ref, dv_ref, *, query_group, query_blocks, key_offset):
    scale = HEAD_SIZE ** (-0.5)
    window = DOC_MOST * BLK
    dk_ref[...] = jnp.zeros_like(dk_ref)
    dv_ref[...] = jnp.zeros_like(dv_ref)
    for qb in range(query_blocks):
        rows = pl.ds(qb * BLK, BLK)
        k0 = key_offset + (qb + 1 - DOC_MOST) * BLK
        kwin = k_ref[pl.ds(k0, window), :]
        vwin = v_ref[pl.ds(k0, window), :]
        qs = jnp.concatenate(
            [q_ref[rows, pl.ds(r * HEAD_SIZE, HEAD_SIZE)] for r in range(query_group)], axis=0)
        dos = jnp.concatenate(
            [do_ref[rows, pl.ds(r * HEAD_SIZE, HEAD_SIZE)] for r in range(query_group)], axis=0)
        outs = jnp.concatenate(
            [o_ref[rows, pl.ds(r * HEAD_SIZE, HEAD_SIZE)] for r in range(query_group)], axis=0)
        delta = jnp.sum(dos.astype(jnp.float32) * outs.astype(jnp.float32), axis=1, keepdims=True)
        qd = qdoc_ref[rows, :]
        kd = kdoc_ref[:, pl.ds(k0, window)]
        qpos = lax.broadcasted_iota(jnp.int32, (BLK, window), 0) + (key_offset + qb * BLK)
        kpos = lax.broadcasted_iota(jnp.int32, (BLK, window), 1) + k0
        allowed = (qd == kd) & (kpos <= qpos)
        mask = jnp.concatenate([allowed] * query_group, axis=0)
        scores = scale * lax.dot_general(
            qs, kwin, (((1,), (1,)), ((), ())), preferred_element_type=jnp.float32)
        masked = jnp.where(mask, scores, -1e30)
        top = jnp.max(masked, axis=1, keepdims=True)
        total = jnp.sum(jnp.where(mask, jnp.exp(masked - top), 0.0), axis=1, keepdims=True)
        lse = top + jnp.log(total)
        probs = jnp.where(mask, jnp.exp(masked - lse), 0.0)
        dprob = lax.dot_general(
            dos, vwin, (((1,), (1,)), ((), ())), preferred_element_type=jnp.float32)
        dscore = (probs * (dprob - delta)).astype(jnp.bfloat16)
        dq = scale * jnp.dot(dscore, kwin, preferred_element_type=jnp.float32)
        for r in range(query_group):
            dq_ref[rows, pl.ds(r * HEAD_SIZE, HEAD_SIZE)] = (
                dq[r * BLK:(r + 1) * BLK].astype(dq_ref.dtype))
        dk_ref[pl.ds(k0, window), :] += scale * lax.dot_general(
            dscore, qs, (((0,), (0,)), ((), ())), preferred_element_type=jnp.float32)
        dv_ref[pl.ds(k0, window), :] += lax.dot_general(
            probs.astype(jnp.bfloat16), dos, (((0,), (0,)), ((), ())),
            preferred_element_type=jnp.float32)


def local_backward(qdoc, kdoc, queries, grads, outputs, keys, values):
    rows, q_cols = queries.shape
    key_rows, kv_cols = keys.shape
    kv_heads = kv_cols // HEAD_SIZE
    query_group = q_cols // HEAD_SIZE // kv_heads
    group_cols = query_group * HEAD_SIZE
    kernel = functools.partial(
        attention_kernel, query_group=query_group, query_blocks=rows // BLK,
        key_offset=key_rows - rows)
    q_spec = pl.BlockSpec((rows, group_cols), lambda g: (0, g))
    k_spec = pl.BlockSpec((key_rows, HEAD_SIZE), lambda g: (0, g))
    return pl.pallas_call(
        kernel,
        grid=(kv_heads,),
        in_specs=[
            pl.BlockSpec((rows, 1), lambda g: (0, 0)),
            pl.BlockSpec((1, key_rows), lambda g: (0, 0)),
            q_spec, q_spec, q_spec, k_spec, k_spec,
        ],
        out_specs=[q_spec, k_spec, k_spec],
        out_shape=[
            jax.ShapeDtypeStruct((rows, q_cols), jnp.bfloat16),
            jax.ShapeDtypeStruct((key_rows, kv_cols), jnp.float32),
            jax.ShapeDtypeStruct((key_rows, kv_cols), jnp.float32),
        ],
        compiler_params=pltpu.CompilerParams(
            dimension_semantics=("arbitrary",), vmem_limit_bytes=48 * 1024 * 1024),
    )(qdoc, kdoc, queries, grads, outputs, keys, values)


def per_device(query_matrix, key_matrix, value_matrix, fwd_output, output_gradient, block_docs):
    queries, key_part, value_part, grads, outputs = (
        lax.all_to_all(query_matrix, "head", split_axis=1, concat_axis=0, tiled=True),
        lax.all_to_all(key_matrix, "head", split_axis=1, concat_axis=0, tiled=True),
        lax.all_to_all(value_matrix, "head", split_axis=1, concat_axis=0, tiled=True),
        lax.all_to_all(output_gradient, "head", split_axis=1, concat_axis=0, tiled=True),
        lax.all_to_all(fwd_output, "head", split_axis=1, concat_axis=0, tiled=True),
    )
    window_extent = queries.shape[0]
    kv_cols = key_part.shape[1]
    place = lax.axis_index("ctx")
    blocks_here = window_extent // BLK

    def docs_of(owner):
        docs = lax.dynamic_slice_in_dim(block_docs, jnp.maximum(owner, 0) * blocks_here, blocks_here, 0)
        return jnp.where(owner >= 0, docs, -1)

    pair = jnp.concatenate([key_part, value_part], axis=1)
    behind = [shifted(pair, "ctx", distance) for distance in range(REACH, 0, -1)]
    keys = jnp.concatenate([b[:, :kv_cols] for b in behind] + [key_part], axis=0)
    values = jnp.concatenate([b[:, kv_cols:] for b in behind] + [value_part], axis=0)
    key_docs = jnp.concatenate([docs_of(place - distance) for distance in range(REACH, -1, -1)])
    kdoc = jnp.repeat(key_docs, BLK)[None, :]
    qdoc = jnp.repeat(docs_of(place), BLK)[:, None]

    query_sum, key_partial, value_partial = local_backward(
        qdoc, kdoc, queries, grads, outputs, keys, values)

    both = jnp.concatenate([key_partial, value_partial], axis=1)
    total = both[REACH * window_extent:]
    for distance in range(1, REACH + 1):
        begin = (REACH - distance) * window_extent
        total = total + shifted(both[begin:begin + window_extent], "ctx", -distance)
    key_sum = total[:, :kv_cols].astype(jnp.bfloat16)
    value_sum = total[:, kv_cols:].astype(jnp.bfloat16)
    return (
        lax.all_to_all(query_sum, "head", split_axis=0, concat_axis=1, tiled=True),
        lax.all_to_all(key_sum, "head", split_axis=0, concat_axis=1, tiled=True),
        lax.all_to_all(value_sum, "head", split_axis=0, concat_axis=1, tiled=True),
    )


def solution(mesh):
    return jax.shard_map(
        per_device,
        mesh=mesh,
        in_specs=(
            P(("groups", "ctx", "head"), None),
            P(("groups", "ctx", "head"), None),
            P(("groups", "ctx", "head"), None),
            P(("groups", "ctx", "head"), None),
            P(("groups", "ctx", "head"), None),
            P("groups"),
        ),
        out_specs=(
            P(("groups", "ctx", "head"), None),
            P(("groups", "ctx", "head"), None),
            P(("groups", "ctx", "head"), None),
        ),
        check_vma=False,
    )
```

```python
import functools

import jax
import jax.numpy as jnp
from jax import lax
from jax.experimental import pallas as pl
from jax.experimental.pallas import tpu as pltpu
from jax.sharding import PartitionSpec as P

HEAD_SIZE = 128
BLK = 128
REACH = 2
DOC_MOST = 6


def shifted(block, axis, distance):
    devices = range(lax.axis_size(axis))
    route = [(i - distance, i) for i in devices if i - distance in devices]
    return lax.ppermute(block, axis, route)


def attention_kernel(qdoc_ref, kdoc_ref, q_ref, do_ref, delta_ref, k_ref, v_ref,
                     dq_ref, dk_ref, dv_ref, *, query_group, query_blocks, key_offset):
    scale = HEAD_SIZE ** (-0.5)
    window = DOC_MOST * BLK
    dk_ref[...] = jnp.zeros_like(dk_ref)
    dv_ref[...] = jnp.zeros_like(dv_ref)
    for qb in range(query_blocks):
        rows = pl.ds(qb * BLK, BLK)
        k0 = key_offset + (qb + 1 - DOC_MOST) * BLK
        kwin = k_ref[pl.ds(k0, window), :]
        vwin = v_ref[pl.ds(k0, window), :]
        qs = jnp.concatenate(
            [q_ref[rows, pl.ds(r * HEAD_SIZE, HEAD_SIZE)] for r in range(query_group)], axis=0)
        dos = jnp.concatenate(
            [do_ref[rows, pl.ds(r * HEAD_SIZE, HEAD_SIZE)] for r in range(query_group)], axis=0)
        delta = jnp.concatenate(
            [delta_ref[0, rows, pl.ds(r, 1)] for r in range(query_group)], axis=0)
        qd = qdoc_ref[rows, :]
        kd = kdoc_ref[:, pl.ds(k0, window)]
        qpos = lax.broadcasted_iota(jnp.int32, (BLK, window), 0) + (key_offset + qb * BLK)
        kpos = lax.broadcasted_iota(jnp.int32, (BLK, window), 1) + k0
        allowed = (qd == kd) & (kpos <= qpos)
        mask = jnp.concatenate([allowed] * query_group, axis=0)
        scores = scale * lax.dot_general(
            qs, kwin, (((1,), (1,)), ((), ())), preferred_element_type=jnp.float32)
        masked = jnp.where(mask, scores, -1e30)
        top = jnp.max(masked, axis=1, keepdims=True)
        total = jnp.sum(jnp.where(mask, jnp.exp(masked - top), 0.0), axis=1, keepdims=True)
        lse = top + jnp.log(total)
        probs = jnp.where(mask, jnp.exp(masked - lse), 0.0)
        dprob = lax.dot_general(
            dos, vwin, (((1,), (1,)), ((), ())), preferred_element_type=jnp.float32)
        dscore = (probs * (dprob - delta)).astype(jnp.bfloat16)
        dq = scale * jnp.dot(dscore, kwin, preferred_element_type=jnp.float32)
        for r in range(query_group):
            dq_ref[rows, pl.ds(r * HEAD_SIZE, HEAD_SIZE)] = (
                dq[r * BLK:(r + 1) * BLK].astype(dq_ref.dtype))
        dk_ref[pl.ds(k0, window), :] += scale * lax.dot_general(
            dscore, qs, (((0,), (0,)), ((), ())), preferred_element_type=jnp.float32)
        dv_ref[pl.ds(k0, window), :] += lax.dot_general(
            probs.astype(jnp.bfloat16), dos, (((0,), (0,)), ((), ())),
            preferred_element_type=jnp.float32)


def local_backward(qdoc, kdoc, queries, grads, delta, keys, values):
    rows, q_cols = queries.shape
    key_rows, kv_cols = keys.shape
    kv_heads = kv_cols // HEAD_SIZE
    query_group = q_cols // HEAD_SIZE // kv_heads
    group_cols = query_group * HEAD_SIZE
    kernel = functools.partial(
        attention_kernel, query_group=query_group, query_blocks=rows // BLK,
        key_offset=key_rows - rows)
    q_spec = pl.BlockSpec((rows, group_cols), lambda g: (0, g))
    k_spec = pl.BlockSpec((key_rows, HEAD_SIZE), lambda g: (0, g))
    return pl.pallas_call(
        kernel,
        grid=(kv_heads,),
        in_specs=[
            pl.BlockSpec((rows, 1), lambda g: (0, 0)),
            pl.BlockSpec((1, key_rows), lambda g: (0, 0)),
            q_spec, q_spec,
            pl.BlockSpec((1, rows, query_group), lambda g: (g, 0, 0)),
            k_spec, k_spec,
        ],
        out_specs=[q_spec, k_spec, k_spec],
        out_shape=[
            jax.ShapeDtypeStruct((rows, q_cols), jnp.bfloat16),
            jax.ShapeDtypeStruct((key_rows, kv_cols), jnp.float32),
            jax.ShapeDtypeStruct((key_rows, kv_cols), jnp.float32),
        ],
        compiler_params=pltpu.CompilerParams(
            dimension_semantics=("arbitrary",), vmem_limit_bytes=48 * 1024 * 1024),
    )(qdoc, kdoc, queries, grads, delta, keys, values)


def per_device(query_matrix, key_matrix, value_matrix, fwd_output, output_gradient, block_docs):
    tokens, q_cols = query_matrix.shape
    all_heads = q_cols // HEAD_SIZE
    delta_here = jnp.sum(
        output_gradient.reshape(tokens, all_heads, HEAD_SIZE).astype(jnp.float32)
        * fwd_output.reshape(tokens, all_heads, HEAD_SIZE).astype(jnp.float32),
        axis=2,
    )
    queries, key_part, value_part, grads, delta_heads = (
        lax.all_to_all(query_matrix, "head", split_axis=1, concat_axis=0, tiled=True),
        lax.all_to_all(key_matrix, "head", split_axis=1, concat_axis=0, tiled=True),
        lax.all_to_all(value_matrix, "head", split_axis=1, concat_axis=0, tiled=True),
        lax.all_to_all(output_gradient, "head", split_axis=1, concat_axis=0, tiled=True),
        lax.all_to_all(delta_here, "head", split_axis=1, concat_axis=0, tiled=True),
    )
    window_extent = queries.shape[0]
    kv_cols = key_part.shape[1]
    kv_heads = kv_cols // HEAD_SIZE
    delta = jnp.transpose(
        delta_heads.reshape(window_extent, kv_heads, delta_heads.shape[1] // kv_heads), (1, 0, 2))
    place = lax.axis_index("ctx")
    blocks_here = window_extent // BLK

    def docs_of(owner):
        docs = lax.dynamic_slice_in_dim(block_docs, jnp.maximum(owner, 0) * blocks_here, blocks_here, 0)
        return jnp.where(owner >= 0, docs, -1)

    pair = jnp.concatenate([key_part, value_part], axis=1)
    behind = [shifted(pair, "ctx", distance) for distance in range(REACH, 0, -1)]
    keys = jnp.concatenate([b[:, :kv_cols] for b in behind] + [key_part], axis=0)
    values = jnp.concatenate([b[:, kv_cols:] for b in behind] + [value_part], axis=0)
    key_docs = jnp.concatenate([docs_of(place - distance) for distance in range(REACH, -1, -1)])
    kdoc = jnp.repeat(key_docs, BLK)[None, :]
    qdoc = jnp.repeat(docs_of(place), BLK)[:, None]

    query_sum, key_partial, value_partial = local_backward(
        qdoc, kdoc, queries, grads, delta, keys, values)

    both = jnp.concatenate([key_partial, value_partial], axis=1)
    own = REACH * window_extent
    total = both[own:]
    reached = own + BLK - DOC_MOST * BLK
    for distance in range(1, REACH + 1):
        begin = (REACH - distance) * window_extent
        start = max(begin, reached)
        if start >= begin + window_extent:
            continue
        sent = shifted(both[start:begin + window_extent].astype(jnp.bfloat16), "ctx", -distance)
        total = total.at[start - begin:].add(sent.astype(jnp.float32))
    key_sum = total[:, :kv_cols].astype(jnp.bfloat16)
    value_sum = total[:, kv_cols:].astype(jnp.bfloat16)
    return (
        lax.all_to_all(query_sum, "head", split_axis=0, concat_axis=1, tiled=True),
        lax.all_to_all(key_sum, "head", split_axis=0, concat_axis=1, tiled=True),
        lax.all_to_all(value_sum, "head", split_axis=0, concat_axis=1, tiled=True),
    )


def solution(mesh):
    return jax.shard_map(
        per_device,
        mesh=mesh,
        in_specs=(
            P(("groups", "ctx", "head"), None),
            P(("groups", "ctx", "head"), None),
            P(("groups", "ctx", "head"), None),
            P(("groups", "ctx", "head"), None),
            P(("groups", "ctx", "head"), None),
            P("groups"),
        ),
        out_specs=(
            P(("groups", "ctx", "head"), None),
            P(("groups", "ctx", "head"), None),
            P(("groups", "ctx", "head"), None),
        ),
        check_vma=False,
    )
```

```python
import functools

import jax
import jax.numpy as jnp
from jax import lax
from jax.experimental import pallas as pl
from jax.experimental.pallas import tpu as pltpu
from jax.sharding import PartitionSpec as P

HEAD_SIZE = 128
BLK = 128
REACH = 2
DOC_MOST = 6
CHUNKS = 2


def shifted(block, axis, distance):
    devices = range(lax.axis_size(axis))
    route = [(i - distance, i) for i in devices if i - distance in devices]
    return lax.ppermute(block, axis, route)


def attention_kernel(qdoc_ref, kdoc_ref, q_ref, do_ref, delta_ref, k_ref, v_ref,
                     dq_ref, dk_ref, dv_ref, *, query_group, query_blocks, key_offset):
    scale = HEAD_SIZE ** (-0.5)
    window = DOC_MOST * BLK
    dk_ref[...] = jnp.zeros_like(dk_ref)
    dv_ref[...] = jnp.zeros_like(dv_ref)
    for qb in range(query_blocks):
        rows = pl.ds(qb * BLK, BLK)
        k0 = key_offset + (qb + 1 - DOC_MOST) * BLK
        kwin = k_ref[pl.ds(k0, window), :]
        vwin = v_ref[pl.ds(k0, window), :]
        qs = jnp.concatenate(
            [q_ref[rows, pl.ds(r * HEAD_SIZE, HEAD_SIZE)] for r in range(query_group)], axis=0)
        dos = jnp.concatenate(
            [do_ref[rows, pl.ds(r * HEAD_SIZE, HEAD_SIZE)] for r in range(query_group)], axis=0)
        delta = jnp.concatenate(
            [delta_ref[0, rows, pl.ds(r, 1)] for r in range(query_group)], axis=0)
        qd = qdoc_ref[rows, :]
        kd = kdoc_ref[:, pl.ds(k0, window)]
        qpos = lax.broadcasted_iota(jnp.int32, (BLK, window), 0) + (key_offset + qb * BLK)
        kpos = lax.broadcasted_iota(jnp.int32, (BLK, window), 1) + k0
        allowed = (qd == kd) & (kpos <= qpos)
        mask = jnp.concatenate([allowed] * query_group, axis=0)
        scores = scale * lax.dot_general(
            qs, kwin, (((1,), (1,)), ((), ())), preferred_element_type=jnp.float32)
        masked = jnp.where(mask, scores, -1e30)
        top = jnp.max(masked, axis=1, keepdims=True)
        total = jnp.sum(jnp.where(mask, jnp.exp(masked - top), 0.0), axis=1, keepdims=True)
        lse = top + jnp.log(total)
        probs = jnp.where(mask, jnp.exp(masked - lse), 0.0)
        dprob = lax.dot_general(
            dos, vwin, (((1,), (1,)), ((), ())), preferred_element_type=jnp.float32)
        dscore = (probs * (dprob - delta)).astype(jnp.bfloat16)
        dq = scale * jnp.dot(dscore, kwin, preferred_element_type=jnp.float32)
        for r in range(query_group):
            dq_ref[rows, pl.ds(r * HEAD_SIZE, HEAD_SIZE)] = (
                dq[r * BLK:(r + 1) * BLK].astype(dq_ref.dtype))
        dk_ref[pl.ds(k0, window), :] += scale * lax.dot_general(
            dscore, qs, (((0,), (0,)), ((), ())), preferred_element_type=jnp.float32)
        dv_ref[pl.ds(k0, window), :] += lax.dot_general(
            probs.astype(jnp.bfloat16), dos, (((0,), (0,)), ((), ())),
            preferred_element_type=jnp.float32)


def local_backward(qdoc, kdoc, queries, grads, delta, keys, values):
    rows, q_cols = queries.shape
    key_rows, kv_cols = keys.shape
    kv_heads = kv_cols // HEAD_SIZE
    query_group = q_cols // HEAD_SIZE // kv_heads
    group_cols = query_group * HEAD_SIZE
    kernel = functools.partial(
        attention_kernel, query_group=query_group, query_blocks=rows // BLK,
        key_offset=key_rows - rows)
    q_spec = pl.BlockSpec((rows, group_cols), lambda g: (0, g))
    k_spec = pl.BlockSpec((key_rows, HEAD_SIZE), lambda g: (0, g))
    return pl.pallas_call(
        kernel,
        grid=(kv_heads,),
        in_specs=[
            pl.BlockSpec((rows, 1), lambda g: (0, 0)),
            pl.BlockSpec((1, key_rows), lambda g: (0, 0)),
            q_spec, q_spec,
            pl.BlockSpec((1, rows, query_group), lambda g: (g, 0, 0)),
            k_spec, k_spec,
        ],
        out_specs=[q_spec, k_spec, k_spec],
        out_shape=[
            jax.ShapeDtypeStruct((rows, q_cols), jnp.bfloat16),
            jax.ShapeDtypeStruct((key_rows, kv_cols), jnp.float32),
            jax.ShapeDtypeStruct((key_rows, kv_cols), jnp.float32),
        ],
        compiler_params=pltpu.CompilerParams(
            dimension_semantics=("arbitrary",), vmem_limit_bytes=48 * 1024 * 1024),
    )(qdoc, kdoc, queries, grads, delta, keys, values)


def per_device(query_matrix, key_matrix, value_matrix, fwd_output, output_gradient, block_docs):
    tokens, q_cols = query_matrix.shape
    kv_all = key_matrix.shape[1]
    all_heads = q_cols // HEAD_SIZE
    peers = lax.axis_size("head")
    delta_here = jnp.sum(
        output_gradient.reshape(tokens, all_heads, HEAD_SIZE).astype(jnp.float32)
        * fwd_output.reshape(tokens, all_heads, HEAD_SIZE).astype(jnp.float32),
        axis=2,
    )
    window_extent = tokens * peers
    place = lax.axis_index("ctx")
    blocks_here = window_extent // BLK
    own = REACH * window_extent
    skip = own + BLK - DOC_MOST * BLK

    def docs_of(owner):
        docs = lax.dynamic_slice_in_dim(block_docs, jnp.maximum(owner, 0) * blocks_here, blocks_here, 0)
        return jnp.where(owner >= 0, docs, -1)

    key_docs = jnp.concatenate([docs_of(place - distance) for distance in range(REACH, -1, -1)])
    kdoc = jnp.repeat(key_docs, BLK)[skip:][None, :]
    qdoc = jnp.repeat(docs_of(place), BLK)[:, None]

    def chunk_of(x, j):
        rows, cols = x.shape
        per = cols // peers // CHUNKS
        return x.reshape(rows, peers, CHUNKS, per)[:, :, j, :].reshape(rows, peers * per)

    def exchange(x):
        return lax.all_to_all(x, "head", split_axis=1, concat_axis=0, tiled=True)

    q_parts, k_parts, v_parts = [], [], []
    for j in range(CHUNKS):
        with jax.named_scope(f"chunk{j}"):
            queries = exchange(chunk_of(query_matrix, j))
            grads = exchange(chunk_of(output_gradient, j))
            key_part = exchange(chunk_of(key_matrix, j))
            value_part = exchange(chunk_of(value_matrix, j))
            delta_heads = exchange(chunk_of(delta_here, j))
            kv_cols = key_part.shape[1]
            kv_heads = kv_cols // HEAD_SIZE
            delta = jnp.transpose(
                delta_heads.reshape(window_extent, kv_heads, delta_heads.shape[1] // kv_heads),
                (1, 0, 2))
            pair = jnp.concatenate([key_part, value_part], axis=1)
            behind = []
            for distance in range(REACH, 0, -1):
                begin = (REACH - distance) * window_extent
                first = max(skip - begin, 0)
                if first < window_extent:
                    behind.append(shifted(pair[first:], "ctx", distance))
            keys = jnp.concatenate([b[:, :kv_cols] for b in behind] + [key_part], axis=0)
            values = jnp.concatenate([b[:, kv_cols:] for b in behind] + [value_part], axis=0)

            query_sum, key_partial, value_partial = local_backward(
                qdoc, kdoc, queries, grads, delta, keys, values)

            both = jnp.concatenate([key_partial, value_partial], axis=1)
            total = both[own - skip:]
            for distance in range(1, REACH + 1):
                begin = (REACH - distance) * window_extent
                start = max(begin, skip)
                if start >= begin + window_extent:
                    continue
                sent = shifted(
                    both[start - skip:begin + window_extent - skip].astype(jnp.bfloat16),
                    "ctx", -distance)
                total = total.at[start - begin:].add(sent.astype(jnp.float32))
            q_parts.append(query_sum)
            k_parts.append(total[:, :kv_cols].astype(jnp.bfloat16))
            v_parts.append(total[:, kv_cols:].astype(jnp.bfloat16))

    def back(parts):
        return lax.all_to_all(
            jnp.concatenate(parts, axis=1), "head", split_axis=0, concat_axis=1, tiled=True)

    return back(q_parts), back(k_parts), back(v_parts)


def solution(mesh):
    return jax.shard_map(
        per_device,
        mesh=mesh,
        in_specs=(
            P(("groups", "ctx", "head"), None),
            P(("groups", "ctx", "head"), None),
            P(("groups", "ctx", "head"), None),
            P(("groups", "ctx", "head"), None),
            P(("groups", "ctx", "head"), None),
            P("groups"),
        ),
        out_specs=(
            P(("groups", "ctx", "head"), None),
            P(("groups", "ctx", "head"), None),
            P(("groups", "ctx", "head"), None),
        ),
        check_vma=False,
    )
```

```python
import functools

import jax
import jax.numpy as jnp
from jax import lax
from jax.experimental import pallas as pl
from jax.experimental.pallas import tpu as pltpu
from jax.sharding import PartitionSpec as P

HEAD_SIZE = 128
BLK = 128
REACH = 2
DOC_MOST = 6


def shifted(block, axis, distance):
    devices = range(lax.axis_size(axis))
    route = [(i - distance, i) for i in devices if i - distance in devices]
    return lax.ppermute(block, axis, route)


def attention_kernel(qdoc_ref, kdoc_ref, q_ref, do_ref, o_ref, k_ref, v_ref,
                     dq_ref, dk_ref, dv_ref, *, query_group, query_blocks, key_offset):
    scale = HEAD_SIZE ** (-0.5)
    window = DOC_MOST * BLK
    dk_ref[...] = jnp.zeros_like(dk_ref)
    dv_ref[...] = jnp.zeros_like(dv_ref)
    for qb in range(query_blocks):
        rows = pl.ds(qb * BLK, BLK)
        k0 = key_offset + (qb + 1 - DOC_MOST) * BLK
        kwin = k_ref[pl.ds(k0, window), :]
        vwin = v_ref[pl.ds(k0, window), :]
        qs = jnp.concatenate(
            [q_ref[rows, pl.ds(r * HEAD_SIZE, HEAD_SIZE)] for r in range(query_group)], axis=0)
        dos = jnp.concatenate(
            [do_ref[rows, pl.ds(r * HEAD_SIZE, HEAD_SIZE)] for r in range(query_group)], axis=0)
        outs = jnp.concatenate(
            [o_ref[rows, pl.ds(r * HEAD_SIZE, HEAD_SIZE)] for r in range(query_group)], axis=0)
        delta = jnp.sum(dos.astype(jnp.float32) * outs.astype(jnp.float32), axis=1, keepdims=True)
        qd = qdoc_ref[rows, :]
        kd = kdoc_ref[:, pl.ds(k0, window)]
        qpos = lax.broadcasted_iota(jnp.int32, (BLK, window), 0) + (key_offset + qb * BLK)
        kpos = lax.broadcasted_iota(jnp.int32, (BLK, window), 1) + k0
        allowed = (qd == kd) & (kpos <= qpos)
        mask = jnp.concatenate([allowed] * query_group, axis=0)
        scores = scale * lax.dot_general(
            qs, kwin, (((1,), (1,)), ((), ())), preferred_element_type=jnp.float32)
        masked = jnp.where(mask, scores, -1e30)
        top = jnp.max(masked, axis=1, keepdims=True)
        total = jnp.sum(jnp.where(mask, jnp.exp(masked - top), 0.0), axis=1, keepdims=True)
        lse = top + jnp.log(total)
        probs = jnp.where(mask, jnp.exp(masked - lse), 0.0)
        dprob = lax.dot_general(
            dos, vwin, (((1,), (1,)), ((), ())), preferred_element_type=jnp.float32)
        dscore = (probs * (dprob - delta)).astype(jnp.bfloat16)
        dq = scale * jnp.dot(dscore, kwin, preferred_element_type=jnp.float32)
        for r in range(query_group):
            dq_ref[rows, pl.ds(r * HEAD_SIZE, HEAD_SIZE)] = (
                dq[r * BLK:(r + 1) * BLK].astype(dq_ref.dtype))
        dk_ref[pl.ds(k0, window), :] += scale * lax.dot_general(
            dscore, qs, (((0,), (0,)), ((), ())), preferred_element_type=jnp.float32)
        dv_ref[pl.ds(k0, window), :] += lax.dot_general(
            probs.astype(jnp.bfloat16), dos, (((0,), (0,)), ((), ())),
            preferred_element_type=jnp.float32)


def local_backward(qdoc, kdoc, fused, q_cols, keys, values):
    rows = fused.shape[0]
    key_rows, kv_cols = keys.shape
    kv_heads = kv_cols // HEAD_SIZE
    query_group = q_cols // HEAD_SIZE // kv_heads
    group_cols = query_group * HEAD_SIZE
    kernel = functools.partial(
        attention_kernel, query_group=query_group, query_blocks=rows // BLK,
        key_offset=key_rows - rows)

    def section(n):
        return pl.BlockSpec((rows, group_cols), lambda g: (0, n * kv_heads + g))

    k_spec = pl.BlockSpec((key_rows, HEAD_SIZE), lambda g: (0, g))
    return pl.pallas_call(
        kernel,
        grid=(kv_heads,),
        in_specs=[
            pl.BlockSpec((rows, 1), lambda g: (0, 0)),
            pl.BlockSpec((1, key_rows), lambda g: (0, 0)),
            section(0), section(1), section(2), k_spec, k_spec,
        ],
        out_specs=[section(0), k_spec, k_spec],
        out_shape=[
            jax.ShapeDtypeStruct((rows, q_cols), jnp.bfloat16),
            jax.ShapeDtypeStruct((key_rows, kv_cols), jnp.float32),
            jax.ShapeDtypeStruct((key_rows, kv_cols), jnp.float32),
        ],
        compiler_params=pltpu.CompilerParams(
            dimension_semantics=("arbitrary",), vmem_limit_bytes=48 * 1024 * 1024),
    )(qdoc, kdoc, fused, fused, fused, keys, values)


def per_device(query_matrix, key_matrix, value_matrix, fwd_output, output_gradient, block_docs):
    tokens, q_all = query_matrix.shape
    kv_all = key_matrix.shape[1]
    peers = lax.axis_size("head")
    q_cols, kv_cols = q_all // peers, kv_all // peers
    sections = (query_matrix, output_gradient, fwd_output, key_matrix, value_matrix)
    outgoing = jnp.concatenate(
        [x[:, p * (x.shape[1] // peers):(p + 1) * (x.shape[1] // peers)]
         for p in range(peers) for x in sections], axis=1)
    fused = lax.all_to_all(outgoing, "head", split_axis=1, concat_axis=0, tiled=True)
    window_extent = fused.shape[0]
    key_part = fused[:, 3 * q_cols:3 * q_cols + kv_cols]
    value_part = fused[:, 3 * q_cols + kv_cols:]
    place = lax.axis_index("ctx")
    blocks_here = window_extent // BLK
    own = REACH * window_extent
    skip = own + BLK - DOC_MOST * BLK

    def docs_of(owner):
        docs = lax.dynamic_slice_in_dim(block_docs, jnp.maximum(owner, 0) * blocks_here, blocks_here, 0)
        return jnp.where(owner >= 0, docs, -1)

    pair = fused[:, 3 * q_cols:]
    behind = []
    for distance in range(REACH, 0, -1):
        first = max(skip - (REACH - distance) * window_extent, 0)
        if first < window_extent:
            behind.append(shifted(pair[first:], "ctx", distance))
    keys = jnp.concatenate([b[:, :kv_cols] for b in behind] + [key_part], axis=0)
    values = jnp.concatenate([b[:, kv_cols:] for b in behind] + [value_part], axis=0)
    key_docs = jnp.concatenate([docs_of(place - distance) for distance in range(REACH, -1, -1)])
    kdoc = jnp.repeat(key_docs, BLK)[skip:][None, :]
    qdoc = jnp.repeat(docs_of(place), BLK)[:, None]

    query_sum, key_partial, value_partial = local_backward(
        qdoc, kdoc, fused, q_cols, keys, values)

    both = jnp.concatenate([key_partial, value_partial], axis=1)
    total = both[own - skip:]
    for distance in range(1, REACH + 1):
        begin = (REACH - distance) * window_extent
        start = max(begin, skip)
        if start >= begin + window_extent:
            continue
        sent = shifted(
            both[start - skip:begin + window_extent - skip].astype(jnp.bfloat16), "ctx", -distance)
        total = total.at[start - begin:].add(sent.astype(jnp.float32))
    finished = jnp.concatenate([query_sum, total.astype(jnp.bfloat16)], axis=1)
    returned = lax.all_to_all(finished, "head", split_axis=0, concat_axis=1, tiled=True)
    width = finished.shape[1]

    def gather(begin, size):
        return jnp.concatenate(
            [returned[:, p * width + begin:p * width + begin + size] for p in range(peers)], axis=1)

    return gather(0, q_cols), gather(q_cols, kv_cols), gather(q_cols + kv_cols, kv_cols)


def solution(mesh):
    return jax.shard_map(
        per_device,
        mesh=mesh,
        in_specs=(
            P(("groups", "ctx", "head"), None),
            P(("groups", "ctx", "head"), None),
            P(("groups", "ctx", "head"), None),
            P(("groups", "ctx", "head"), None),
            P(("groups", "ctx", "head"), None),
            P("groups"),
        ),
        out_specs=(
            P(("groups", "ctx", "head"), None),
            P(("groups", "ctx", "head"), None),
            P(("groups", "ctx", "head"), None),
        ),
        check_vma=False,
    )
```

```python
import functools

import jax
import jax.numpy as jnp
from jax import lax
from jax.experimental import pallas as pl
from jax.experimental.pallas import tpu as pltpu
from jax.sharding import PartitionSpec as P

HEAD_SIZE = 128
BLK = 128
REACH = 2
DOC_MOST = 6
CHUNKS = 2


def shifted(block, axis, distance):
    devices = range(lax.axis_size(axis))
    route = [(i - distance, i) for i in devices if i - distance in devices]
    return lax.ppermute(block, axis, route)


def attention_kernel(qdoc_ref, kdoc_ref, q_ref, do_ref, o_ref, k_ref, v_ref,
                     dq_ref, dk_ref, dv_ref, *, query_group, query_blocks, key_offset):
    scale = HEAD_SIZE ** (-0.5)
    window = DOC_MOST * BLK
    dk_ref[...] = jnp.zeros_like(dk_ref)
    dv_ref[...] = jnp.zeros_like(dv_ref)
    for qb in range(query_blocks):
        rows = pl.ds(qb * BLK, BLK)
        k0 = key_offset + (qb + 1 - DOC_MOST) * BLK
        kwin = k_ref[pl.ds(k0, window), :]
        vwin = v_ref[pl.ds(k0, window), :]
        qs = jnp.concatenate(
            [q_ref[rows, pl.ds(r * HEAD_SIZE, HEAD_SIZE)] for r in range(query_group)], axis=0)
        dos = jnp.concatenate(
            [do_ref[rows, pl.ds(r * HEAD_SIZE, HEAD_SIZE)] for r in range(query_group)], axis=0)
        outs = jnp.concatenate(
            [o_ref[rows, pl.ds(r * HEAD_SIZE, HEAD_SIZE)] for r in range(query_group)], axis=0)
        delta = jnp.sum(dos.astype(jnp.float32) * outs.astype(jnp.float32), axis=1, keepdims=True)
        qd = qdoc_ref[rows, :]
        kd = kdoc_ref[:, pl.ds(k0, window)]
        qpos = lax.broadcasted_iota(jnp.int32, (BLK, window), 0) + (key_offset + qb * BLK)
        kpos = lax.broadcasted_iota(jnp.int32, (BLK, window), 1) + k0
        allowed = (qd == kd) & (kpos <= qpos)
        mask = jnp.concatenate([allowed] * query_group, axis=0)
        scores = scale * lax.dot_general(
            qs, kwin, (((1,), (1,)), ((), ())), preferred_element_type=jnp.float32)
        masked = jnp.where(mask, scores, -1e30)
        top = jnp.max(masked, axis=1, keepdims=True)
        total = jnp.sum(jnp.where(mask, jnp.exp(masked - top), 0.0), axis=1, keepdims=True)
        lse = top + jnp.log(total)
        probs = jnp.where(mask, jnp.exp(masked - lse), 0.0)
        dprob = lax.dot_general(
            dos, vwin, (((1,), (1,)), ((), ())), preferred_element_type=jnp.float32)
        dscore = (probs * (dprob - delta)).astype(jnp.bfloat16)
        dq = scale * jnp.dot(dscore, kwin, preferred_element_type=jnp.float32)
        for r in range(query_group):
            dq_ref[rows, pl.ds(r * HEAD_SIZE, HEAD_SIZE)] = (
                dq[r * BLK:(r + 1) * BLK].astype(dq_ref.dtype))
        dk_ref[pl.ds(k0, window), :] += scale * lax.dot_general(
            dscore, qs, (((0,), (0,)), ((), ())), preferred_element_type=jnp.float32)
        dv_ref[pl.ds(k0, window), :] += lax.dot_general(
            probs.astype(jnp.bfloat16), dos, (((0,), (0,)), ((), ())),
            preferred_element_type=jnp.float32)


def local_backward(qdoc, kdoc, fused, q_cols, all_kv, head0, keys, values):
    rows = fused.shape[0]
    key_rows, kv_cols = keys.shape
    kv_heads = kv_cols // HEAD_SIZE
    query_group = q_cols // HEAD_SIZE // all_kv
    group_cols = query_group * HEAD_SIZE
    kernel = functools.partial(
        attention_kernel, query_group=query_group, query_blocks=rows // BLK,
        key_offset=key_rows - rows)

    def section(n):
        return pl.BlockSpec((rows, group_cols), lambda g: (0, n * all_kv + head0 + g))

    out_spec = pl.BlockSpec((rows, group_cols), lambda g: (0, g))

    k_spec = pl.BlockSpec((key_rows, HEAD_SIZE), lambda g: (0, g))
    return pl.pallas_call(
        kernel,
        grid=(kv_heads,),
        in_specs=[
            pl.BlockSpec((rows, 1), lambda g: (0, 0)),
            pl.BlockSpec((1, key_rows), lambda g: (0, 0)),
            section(0), section(1), section(2), k_spec, k_spec,
        ],
        out_specs=[out_spec, k_spec, k_spec],
        out_shape=[
            jax.ShapeDtypeStruct((rows, kv_heads * group_cols), jnp.bfloat16),
            jax.ShapeDtypeStruct((key_rows, kv_cols), jnp.float32),
            jax.ShapeDtypeStruct((key_rows, kv_cols), jnp.float32),
        ],
        compiler_params=pltpu.CompilerParams(
            dimension_semantics=("arbitrary",), vmem_limit_bytes=48 * 1024 * 1024),
    )(qdoc, kdoc, fused, fused, fused, keys, values)


def per_device(query_matrix, key_matrix, value_matrix, fwd_output, output_gradient, block_docs):
    tokens, q_all = query_matrix.shape
    kv_all = key_matrix.shape[1]
    peers = lax.axis_size("head")
    q_cols, kv_cols = q_all // peers, kv_all // peers
    sections = (query_matrix, output_gradient, fwd_output, key_matrix, value_matrix)
    outgoing = jnp.concatenate(
        [x[:, p * (x.shape[1] // peers):(p + 1) * (x.shape[1] // peers)]
         for p in range(peers) for x in sections], axis=1)
    fused = lax.all_to_all(outgoing, "head", split_axis=1, concat_axis=0, tiled=True)
    window_extent = fused.shape[0]
    key_part = fused[:, 3 * q_cols:3 * q_cols + kv_cols]
    value_part = fused[:, 3 * q_cols + kv_cols:]
    place = lax.axis_index("ctx")
    blocks_here = window_extent // BLK
    own = REACH * window_extent
    skip = own + BLK - DOC_MOST * BLK

    def docs_of(owner):
        docs = lax.dynamic_slice_in_dim(block_docs, jnp.maximum(owner, 0) * blocks_here, blocks_here, 0)
        return jnp.where(owner >= 0, docs, -1)

    key_docs = jnp.concatenate([docs_of(place - distance) for distance in range(REACH, -1, -1)])
    kdoc = jnp.repeat(key_docs, BLK)[skip:][None, :]
    qdoc = jnp.repeat(docs_of(place), BLK)[:, None]
    all_kv = kv_cols // HEAD_SIZE
    per = kv_cols // CHUNKS
    q_parts, k_parts, v_parts = [], [], []
    for j in range(CHUNKS):
        with jax.named_scope(f"chunk{j}"):
            key_here = key_part[:, j * per:(j + 1) * per]
            value_here = value_part[:, j * per:(j + 1) * per]
            pair = jnp.concatenate([key_here, value_here], axis=1)
            behind = []
            for distance in range(REACH, 0, -1):
                first = max(skip - (REACH - distance) * window_extent, 0)
                if first < window_extent:
                    behind.append(shifted(pair[first:], "ctx", distance))
            keys = jnp.concatenate([b[:, :per] for b in behind] + [key_here], axis=0)
            values = jnp.concatenate([b[:, per:] for b in behind] + [value_here], axis=0)

            query_sum, key_partial, value_partial = local_backward(
                qdoc, kdoc, fused, q_cols, all_kv, j * per // HEAD_SIZE, keys, values)

            both = jnp.concatenate([key_partial, value_partial], axis=1)
            total = both[own - skip:]
            for distance in range(1, REACH + 1):
                begin = (REACH - distance) * window_extent
                start = max(begin, skip)
                if start >= begin + window_extent:
                    continue
                sent = shifted(
                    both[start - skip:begin + window_extent - skip].astype(jnp.bfloat16),
                    "ctx", -distance)
                total = total.at[start - begin:].add(sent.astype(jnp.float32))
            q_parts.append(query_sum)
            k_parts.append(total[:, :per].astype(jnp.bfloat16))
            v_parts.append(total[:, per:].astype(jnp.bfloat16))
    finished = jnp.concatenate(q_parts + k_parts + v_parts, axis=1)
    returned = lax.all_to_all(finished, "head", split_axis=0, concat_axis=1, tiled=True)
    width = finished.shape[1]

    def gather(begin, size):
        return jnp.concatenate(
            [returned[:, p * width + begin:p * width + begin + size] for p in range(peers)], axis=1)

    return gather(0, q_cols), gather(q_cols, kv_cols), gather(q_cols + kv_cols, kv_cols)


def solution(mesh):
    return jax.shard_map(
        per_device,
        mesh=mesh,
        in_specs=(
            P(("groups", "ctx", "head"), None),
            P(("groups", "ctx", "head"), None),
            P(("groups", "ctx", "head"), None),
            P(("groups", "ctx", "head"), None),
            P(("groups", "ctx", "head"), None),
            P("groups"),
        ),
        out_specs=(
            P(("groups", "ctx", "head"), None),
            P(("groups", "ctx", "head"), None),
            P(("groups", "ctx", "head"), None),
        ),
        check_vma=False,
    )
```

```python
import functools

import jax
import jax.numpy as jnp
from jax import lax
from jax.experimental import pallas as pl
from jax.experimental.pallas import tpu as pltpu
from jax.sharding import PartitionSpec as P

HEAD_SIZE = 128
BLK = 128
REACH = 2
DOC_MOST = 6
CHUNKS = 2


def shifted(block, axis, distance):
    devices = range(lax.axis_size(axis))
    route = [(i - distance, i) for i in devices if i - distance in devices]
    return lax.ppermute(block, axis, route)


def attention_kernel(bdoc_ref, qdoc_ref, kdoc_ref, q_ref, do_ref, o_ref, k_ref, v_ref,
                     dq_ref, dk_ref, dv_ref, s_scr, m_scr, l_scr, dq_scr,
                     *, query_group, query_blocks, key_offset):
    scale = HEAD_SIZE ** (-0.5)
    dk_ref[...] = jnp.zeros_like(dk_ref)
    dv_ref[...] = jnp.zeros_like(dv_ref)
    for qb in range(query_blocks):
        rows = pl.ds(qb * BLK, BLK)
        first = key_offset // BLK + qb + 1 - DOC_MOST
        qs = jnp.concatenate(
            [q_ref[rows, pl.ds(r * HEAD_SIZE, HEAD_SIZE)] for r in range(query_group)], axis=0)
        dos = jnp.concatenate(
            [do_ref[rows, pl.ds(r * HEAD_SIZE, HEAD_SIZE)] for r in range(query_group)], axis=0)
        outs = jnp.concatenate(
            [o_ref[rows, pl.ds(r * HEAD_SIZE, HEAD_SIZE)] for r in range(query_group)], axis=0)
        delta = jnp.sum(dos.astype(jnp.float32) * outs.astype(jnp.float32), axis=1, keepdims=True)
        qd = qdoc_ref[rows, :]
        query_doc = bdoc_ref[qb]

        def mask_of(kb):
            kd = kdoc_ref[:, pl.ds(kb * BLK, BLK)]
            qpos = lax.broadcasted_iota(jnp.int32, (BLK, BLK), 0) + (key_offset + qb * BLK)
            kpos = lax.broadcasted_iota(jnp.int32, (BLK, BLK), 1) + kb * BLK
            allowed = (qd == kd) & (kpos <= qpos)
            return jnp.concatenate([allowed] * query_group, axis=0)

        m_scr[...] = jnp.full(m_scr.shape, -1e30, jnp.float32)
        l_scr[...] = jnp.zeros(l_scr.shape, jnp.float32)
        dq_scr[...] = jnp.zeros(dq_scr.shape, jnp.float32)
        for b in range(DOC_MOST):
            kb = first + b

            @pl.when(bdoc_ref[query_blocks + kb] == query_doc)
            def _():
                kblk = k_ref[pl.ds(kb * BLK, BLK), :]
                scores = scale * lax.dot_general(
                    qs, kblk, (((1,), (1,)), ((), ())), preferred_element_type=jnp.float32)
                masked = jnp.where(mask_of(kb), scores, -1e30)
                s_scr[b] = masked
                m_scr[...] = jnp.maximum(m_scr[...], jnp.max(masked, axis=1, keepdims=True))

        for b in range(DOC_MOST):
            kb = first + b

            @pl.when(bdoc_ref[query_blocks + kb] == query_doc)
            def _():
                l_scr[...] += jnp.sum(
                    jnp.where(mask_of(kb), jnp.exp(s_scr[b] - m_scr[...]), 0.0),
                    axis=1, keepdims=True)

        lse = m_scr[...] + jnp.log(l_scr[...])
        for b in range(DOC_MOST):
            kb = first + b

            @pl.when(bdoc_ref[query_blocks + kb] == query_doc)
            def _():
                kblk = k_ref[pl.ds(kb * BLK, BLK), :]
                vblk = v_ref[pl.ds(kb * BLK, BLK), :]
                probs = jnp.where(mask_of(kb), jnp.exp(s_scr[b] - lse), 0.0)
                dprob = lax.dot_general(
                    dos, vblk, (((1,), (1,)), ((), ())), preferred_element_type=jnp.float32)
                dscore = (probs * (dprob - delta)).astype(jnp.bfloat16)
                dq_scr[...] += jnp.dot(dscore, kblk, preferred_element_type=jnp.float32)
                dk_ref[pl.ds(kb * BLK, BLK), :] += scale * lax.dot_general(
                    dscore, qs, (((0,), (0,)), ((), ())), preferred_element_type=jnp.float32)
                dv_ref[pl.ds(kb * BLK, BLK), :] += lax.dot_general(
                    probs.astype(jnp.bfloat16), dos, (((0,), (0,)), ((), ())),
                    preferred_element_type=jnp.float32)

        dq = scale * dq_scr[...]
        for r in range(query_group):
            dq_ref[rows, pl.ds(r * HEAD_SIZE, HEAD_SIZE)] = (
                dq[r * BLK:(r + 1) * BLK].astype(dq_ref.dtype))


def local_backward(bdoc, qdoc, kdoc, fused, q_cols, all_kv, head0, keys, values):
    rows = fused.shape[0]
    key_rows, kv_cols = keys.shape
    kv_heads = kv_cols // HEAD_SIZE
    query_group = q_cols // HEAD_SIZE // all_kv
    group_cols = query_group * HEAD_SIZE
    kernel = functools.partial(
        attention_kernel, query_group=query_group, query_blocks=rows // BLK,
        key_offset=key_rows - rows)

    def section(n):
        return pl.BlockSpec((rows, group_cols), lambda g, bd: (0, n * all_kv + head0 + g))

    out_spec = pl.BlockSpec((rows, group_cols), lambda g, bd: (0, g))

    k_spec = pl.BlockSpec((key_rows, HEAD_SIZE), lambda g, bd: (0, g))
    stacked = query_group * BLK
    grid_spec = pltpu.PrefetchScalarGridSpec(
        num_scalar_prefetch=1,
        grid=(kv_heads,),
        in_specs=[
            pl.BlockSpec((rows, 1), lambda g, bd: (0, 0)),
            pl.BlockSpec((1, key_rows), lambda g, bd: (0, 0)),
            section(0), section(1), section(2), k_spec, k_spec,
        ],
        out_specs=[out_spec, k_spec, k_spec],
        scratch_shapes=[
            pltpu.VMEM((DOC_MOST, stacked, BLK), jnp.float32),
            pltpu.VMEM((stacked, 1), jnp.float32),
            pltpu.VMEM((stacked, 1), jnp.float32),
            pltpu.VMEM((stacked, HEAD_SIZE), jnp.float32),
        ],
    )
    return pl.pallas_call(
        kernel,
        grid_spec=grid_spec,
        out_shape=[
            jax.ShapeDtypeStruct((rows, kv_heads * group_cols), jnp.bfloat16),
            jax.ShapeDtypeStruct((key_rows, kv_cols), jnp.float32),
            jax.ShapeDtypeStruct((key_rows, kv_cols), jnp.float32),
        ],
        compiler_params=pltpu.CompilerParams(
            dimension_semantics=("arbitrary",), vmem_limit_bytes=48 * 1024 * 1024),
    )(bdoc, qdoc, kdoc, fused, fused, fused, keys, values)


def per_device(query_matrix, key_matrix, value_matrix, fwd_output, output_gradient, block_docs):
    _, q_all = query_matrix.shape
    kv_all = key_matrix.shape[1]
    peers = lax.axis_size("head")
    q_cols, kv_cols = q_all // peers, kv_all // peers
    sections = (query_matrix, output_gradient, fwd_output, key_matrix, value_matrix)
    outgoing = jnp.concatenate(
        [x[:, p * (x.shape[1] // peers):(p + 1) * (x.shape[1] // peers)]
         for p in range(peers) for x in sections], axis=1)
    fused = lax.all_to_all(outgoing, "head", split_axis=1, concat_axis=0, tiled=True)
    window_extent = fused.shape[0]
    key_part = fused[:, 3 * q_cols:3 * q_cols + kv_cols]
    value_part = fused[:, 3 * q_cols + kv_cols:]
    place = lax.axis_index("ctx")
    blocks_here = window_extent // BLK
    own = REACH * window_extent
    skip = own + BLK - DOC_MOST * BLK

    def docs_of(owner):
        docs = lax.dynamic_slice_in_dim(block_docs, jnp.maximum(owner, 0) * blocks_here, blocks_here, 0)
        return jnp.where(owner >= 0, docs, -1)

    key_docs = jnp.concatenate([docs_of(place - distance) for distance in range(REACH, -1, -1)])
    kdoc = jnp.repeat(key_docs, BLK)[skip:][None, :]
    qdoc = jnp.repeat(docs_of(place), BLK)[:, None]
    bdoc = jnp.concatenate([docs_of(place), key_docs[skip // BLK:]])
    all_kv = kv_cols // HEAD_SIZE
    per = kv_cols // CHUNKS
    q_parts, k_parts, v_parts = [], [], []
    for j in range(CHUNKS):
        key_here = key_part[:, j * per:(j + 1) * per]
        value_here = value_part[:, j * per:(j + 1) * per]
        pair = jnp.concatenate([key_here, value_here], axis=1)
        behind = []
        for distance in range(REACH, 0, -1):
            first = max(skip - (REACH - distance) * window_extent, 0)
            if first < window_extent:
                behind.append(shifted(pair[first:], "ctx", distance))
        keys = jnp.concatenate([b[:, :per] for b in behind] + [key_here], axis=0)
        values = jnp.concatenate([b[:, per:] for b in behind] + [value_here], axis=0)

        query_sum, key_partial, value_partial = local_backward(
            bdoc, qdoc, kdoc, fused, q_cols, all_kv, j * per // HEAD_SIZE, keys, values)

        both = jnp.concatenate([key_partial, value_partial], axis=1)
        total = both[own - skip:]
        for distance in range(1, REACH + 1):
            begin = (REACH - distance) * window_extent
            start = max(begin, skip)
            if start >= begin + window_extent:
                continue
            sent = shifted(
                both[start - skip:begin + window_extent - skip].astype(jnp.bfloat16),
                "ctx", -distance)
            total = total.at[start - begin:].add(sent.astype(jnp.float32))
        q_parts.append(query_sum)
        k_parts.append(total[:, :per].astype(jnp.bfloat16))
        v_parts.append(total[:, per:].astype(jnp.bfloat16))
    finished = jnp.concatenate(q_parts + k_parts + v_parts, axis=1)
    returned = lax.all_to_all(finished, "head", split_axis=0, concat_axis=1, tiled=True)
    width = finished.shape[1]

    def gather(begin, size):
        return jnp.concatenate(
            [returned[:, p * width + begin:p * width + begin + size] for p in range(peers)], axis=1)

    return gather(0, q_cols), gather(q_cols, kv_cols), gather(q_cols + kv_cols, kv_cols)


def solution(mesh):
    return jax.shard_map(
        per_device,
        mesh=mesh,
        in_specs=(
            P(("groups", "ctx", "head"), None),
            P(("groups", "ctx", "head"), None),
            P(("groups", "ctx", "head"), None),
            P(("groups", "ctx", "head"), None),
            P(("groups", "ctx", "head"), None),
            P("groups"),
        ),
        out_specs=(
            P(("groups", "ctx", "head"), None),
            P(("groups", "ctx", "head"), None),
            P(("groups", "ctx", "head"), None),
        ),
        check_vma=False,
    )
```

```python
import functools

import jax
import jax.numpy as jnp
from jax import lax
from jax.experimental import pallas as pl
from jax.experimental.pallas import tpu as pltpu
from jax.sharding import PartitionSpec as P

HEAD_SIZE = 128
BLK = 128
REACH = 2
DOC_MOST = 6
CHUNKS = 2


def shifted(block, axis, distance):
    devices = range(lax.axis_size(axis))
    route = [(i - distance, i) for i in devices if i - distance in devices]
    return lax.ppermute(block, axis, route)


def attention_kernel(qdoc_ref, kdoc_ref, q_ref, do_ref, o_ref, k_ref, v_ref,
                     dq_ref, dk_ref, dv_ref, *, query_group, query_blocks, key_offset):
    scale = HEAD_SIZE ** (-0.5)
    window = DOC_MOST * BLK
    dk_ref[...] = jnp.zeros_like(dk_ref)
    dv_ref[...] = jnp.zeros_like(dv_ref)
    for qb in range(query_blocks):
        rows = pl.ds(qb * BLK, BLK)
        k0 = key_offset + (qb + 1 - DOC_MOST) * BLK
        kwin = k_ref[pl.ds(k0, window), :]
        vwin = v_ref[pl.ds(k0, window), :]
        qs = jnp.concatenate(
            [q_ref[rows, pl.ds(r * HEAD_SIZE, HEAD_SIZE)] for r in range(query_group)], axis=0)
        dos = jnp.concatenate(
            [do_ref[rows, pl.ds(r * HEAD_SIZE, HEAD_SIZE)] for r in range(query_group)], axis=0)
        outs = jnp.concatenate(
            [o_ref[rows, pl.ds(r * HEAD_SIZE, HEAD_SIZE)] for r in range(query_group)], axis=0)
        product = dos.astype(jnp.float32) * outs.astype(jnp.float32)
        delta = jnp.sum(product.T, axis=0, keepdims=True)
        qd = qdoc_ref[:, rows]
        kd = kdoc_ref[pl.ds(k0, window), :]
        qpos = lax.broadcasted_iota(jnp.int32, (window, BLK), 1) + (key_offset + qb * BLK)
        kpos = lax.broadcasted_iota(jnp.int32, (window, BLK), 0) + k0
        allowed = (kd == qd) & (kpos <= qpos)
        mask = jnp.concatenate([allowed] * query_group, axis=1)
        scores = scale * lax.dot_general(
            kwin, qs, (((1,), (1,)), ((), ())), preferred_element_type=jnp.float32)
        masked = jnp.where(mask, scores, -1e30)
        top = jnp.max(masked, axis=0, keepdims=True)
        total = jnp.sum(jnp.exp(masked - top), axis=0, keepdims=True)
        lse = top + jnp.log(total)
        probs = jnp.exp(masked - lse)
        dprob = lax.dot_general(
            vwin, dos, (((1,), (1,)), ((), ())), preferred_element_type=jnp.float32)
        dscore = (probs * (dprob - delta)).astype(jnp.bfloat16)
        dq = scale * lax.dot_general(
            dscore, kwin, (((0,), (0,)), ((), ())), preferred_element_type=jnp.float32)
        for r in range(query_group):
            dq_ref[rows, pl.ds(r * HEAD_SIZE, HEAD_SIZE)] = (
                dq[r * BLK:(r + 1) * BLK].astype(dq_ref.dtype))
        dk_ref[pl.ds(k0, window), :] += scale * jnp.dot(
            dscore, qs, preferred_element_type=jnp.float32)
        dv_ref[pl.ds(k0, window), :] += jnp.dot(
            probs.astype(jnp.bfloat16), dos, preferred_element_type=jnp.float32)


def local_backward(qdoc, kdoc, fused, q_cols, all_kv, head0, keys, values):
    rows = fused.shape[0]
    key_rows, kv_cols = keys.shape
    kv_heads = kv_cols // HEAD_SIZE
    query_group = q_cols // HEAD_SIZE // all_kv
    group_cols = query_group * HEAD_SIZE
    kernel = functools.partial(
        attention_kernel, query_group=query_group, query_blocks=rows // BLK,
        key_offset=key_rows - rows)

    def section(n):
        return pl.BlockSpec((rows, group_cols), lambda g: (0, n * all_kv + head0 + g))

    out_spec = pl.BlockSpec((rows, group_cols), lambda g: (0, g))

    k_spec = pl.BlockSpec((key_rows, HEAD_SIZE), lambda g: (0, g))
    return pl.pallas_call(
        kernel,
        grid=(kv_heads,),
        in_specs=[
            pl.BlockSpec((1, rows), lambda g: (0, 0)),
            pl.BlockSpec((key_rows, 1), lambda g: (0, 0)),
            section(0), section(1), section(2), k_spec, k_spec,
        ],
        out_specs=[out_spec, k_spec, k_spec],
        out_shape=[
            jax.ShapeDtypeStruct((rows, kv_heads * group_cols), jnp.bfloat16),
            jax.ShapeDtypeStruct((key_rows, kv_cols), jnp.float32),
            jax.ShapeDtypeStruct((key_rows, kv_cols), jnp.float32),
        ],
        compiler_params=pltpu.CompilerParams(
            dimension_semantics=("arbitrary",), vmem_limit_bytes=48 * 1024 * 1024),
    )(qdoc, kdoc, fused, fused, fused, keys, values)


def per_device(query_matrix, key_matrix, value_matrix, fwd_output, output_gradient, block_docs):
    _, q_all = query_matrix.shape
    kv_all = key_matrix.shape[1]
    peers = lax.axis_size("head")
    q_cols, kv_cols = q_all // peers, kv_all // peers
    sections = (query_matrix, output_gradient, fwd_output, key_matrix, value_matrix)
    outgoing = jnp.concatenate(
        [x[:, p * (x.shape[1] // peers):(p + 1) * (x.shape[1] // peers)]
         for p in range(peers) for x in sections], axis=1)
    fused = lax.all_to_all(outgoing, "head", split_axis=1, concat_axis=0, tiled=True)
    window_extent = fused.shape[0]
    key_part = fused[:, 3 * q_cols:3 * q_cols + kv_cols]
    value_part = fused[:, 3 * q_cols + kv_cols:]
    place = lax.axis_index("ctx")
    blocks_here = window_extent // BLK
    own = REACH * window_extent
    skip = own + BLK - DOC_MOST * BLK

    def docs_of(owner):
        docs = lax.dynamic_slice_in_dim(block_docs, jnp.maximum(owner, 0) * blocks_here, blocks_here, 0)
        return jnp.where(owner >= 0, docs, -1)

    key_docs = jnp.concatenate([docs_of(place - distance) for distance in range(REACH, -1, -1)])
    kdoc = jnp.repeat(key_docs, BLK)[skip:][:, None]
    qdoc = jnp.repeat(docs_of(place), BLK)[None, :]
    all_kv = kv_cols // HEAD_SIZE
    per = kv_cols // CHUNKS
    q_parts, k_parts, v_parts = [], [], []
    for j in range(CHUNKS):
        key_here = key_part[:, j * per:(j + 1) * per]
        value_here = value_part[:, j * per:(j + 1) * per]
        pair = jnp.concatenate([key_here, value_here], axis=1)
        behind = []
        for distance in range(REACH, 0, -1):
            first = max(skip - (REACH - distance) * window_extent, 0)
            if first < window_extent:
                behind.append(shifted(pair[first:], "ctx", distance))
        keys = jnp.concatenate([b[:, :per] for b in behind] + [key_here], axis=0)
        values = jnp.concatenate([b[:, per:] for b in behind] + [value_here], axis=0)

        query_sum, key_partial, value_partial = local_backward(
            qdoc, kdoc, fused, q_cols, all_kv, j * per // HEAD_SIZE, keys, values)

        both = jnp.concatenate([key_partial, value_partial], axis=1)
        total = both[own - skip:]
        for distance in range(1, REACH + 1):
            begin = (REACH - distance) * window_extent
            start = max(begin, skip)
            if start >= begin + window_extent:
                continue
            sent = shifted(
                both[start - skip:begin + window_extent - skip].astype(jnp.bfloat16),
                "ctx", -distance)
            total = total.at[start - begin:].add(sent.astype(jnp.float32))
        q_parts.append(query_sum)
        k_parts.append(total[:, :per].astype(jnp.bfloat16))
        v_parts.append(total[:, per:].astype(jnp.bfloat16))
    finished = jnp.concatenate(q_parts + k_parts + v_parts, axis=1)
    returned = lax.all_to_all(finished, "head", split_axis=0, concat_axis=1, tiled=True)
    width = finished.shape[1]

    def gather(begin, size):
        return jnp.concatenate(
            [returned[:, p * width + begin:p * width + begin + size] for p in range(peers)], axis=1)

    return gather(0, q_cols), gather(q_cols, kv_cols), gather(q_cols + kv_cols, kv_cols)


def solution(mesh):
    return jax.shard_map(
        per_device,
        mesh=mesh,
        in_specs=(
            P(("groups", "ctx", "head"), None),
            P(("groups", "ctx", "head"), None),
            P(("groups", "ctx", "head"), None),
            P(("groups", "ctx", "head"), None),
            P(("groups", "ctx", "head"), None),
            P("groups"),
        ),
        out_specs=(
            P(("groups", "ctx", "head"), None),
            P(("groups", "ctx", "head"), None),
            P(("groups", "ctx", "head"), None),
        ),
        check_vma=False,
    )
```

```python
import functools

import jax
import jax.numpy as jnp
from jax import lax
from jax.experimental import pallas as pl
from jax.experimental.pallas import tpu as pltpu
from jax.sharding import PartitionSpec as P

HEAD_SIZE = 128
BLK = 128
REACH = 2
DOC_MOST = 6
CHUNKS = 2


def shifted(block, axis, distance):
    devices = range(lax.axis_size(axis))
    route = [(i - distance, i) for i in devices if i - distance in devices]
    return lax.ppermute(block, axis, route)


def attention_kernel(qdoc_ref, kdoc_ref, q_ref, do_ref, o_ref, k_ref, v_ref,
                     dq_ref, dk_ref, dv_ref, *, query_group, query_blocks, key_offset):
    scale = HEAD_SIZE ** (-0.5)
    window = DOC_MOST * BLK
    dk_ref[...] = jnp.zeros_like(dk_ref)
    dv_ref[...] = jnp.zeros_like(dv_ref)
    for qb in range(query_blocks):
        rows = pl.ds(qb * BLK, BLK)
        k0 = key_offset + (qb + 1 - DOC_MOST) * BLK
        kwin = k_ref[pl.ds(k0, window), :]
        vwin = v_ref[pl.ds(k0, window), :]
        qs = jnp.concatenate(
            [q_ref[rows, pl.ds(r * HEAD_SIZE, HEAD_SIZE)] for r in range(query_group)], axis=0)
        dos = jnp.concatenate(
            [do_ref[rows, pl.ds(r * HEAD_SIZE, HEAD_SIZE)] for r in range(query_group)], axis=0)
        outs = jnp.concatenate(
            [o_ref[rows, pl.ds(r * HEAD_SIZE, HEAD_SIZE)] for r in range(query_group)], axis=0)
        delta = jnp.sum(dos.astype(jnp.float32) * outs.astype(jnp.float32), axis=1, keepdims=True)
        qd = qdoc_ref[rows, :]
        kd = kdoc_ref[:, pl.ds(k0, window)]
        qpos = lax.broadcasted_iota(jnp.int32, (BLK, window), 0) + (key_offset + qb * BLK)
        kpos = lax.broadcasted_iota(jnp.int32, (BLK, window), 1) + k0
        allowed = (qd == kd) & (kpos <= qpos)
        mask = jnp.concatenate([allowed] * query_group, axis=0)
        scores = scale * lax.dot_general(
            qs, kwin, (((1,), (1,)), ((), ())), preferred_element_type=jnp.float32)
        masked = jnp.where(mask, scores, -1e30)
        top = jnp.max(masked, axis=1, keepdims=True)
        total = jnp.sum(jnp.where(mask, jnp.exp(masked - top), 0.0), axis=1, keepdims=True)
        lse = top + jnp.log(total)
        probs = jnp.where(mask, jnp.exp(masked - lse), 0.0)
        dprob = lax.dot_general(
            dos, vwin, (((1,), (1,)), ((), ())), preferred_element_type=jnp.float32)
        dscore = (probs * (dprob - delta)).astype(jnp.bfloat16)
        dq = scale * jnp.dot(dscore, kwin, preferred_element_type=jnp.float32)
        for r in range(query_group):
            dq_ref[rows, pl.ds(r * HEAD_SIZE, HEAD_SIZE)] = (
                dq[r * BLK:(r + 1) * BLK].astype(dq_ref.dtype))
        dk_ref[pl.ds(k0, window), :] += scale * lax.dot_general(
            dscore, qs, (((0,), (0,)), ((), ())), preferred_element_type=jnp.float32)
        dv_ref[pl.ds(k0, window), :] += lax.dot_general(
            probs.astype(jnp.bfloat16), dos, (((0,), (0,)), ((), ())),
            preferred_element_type=jnp.float32)


def local_backward(qdoc, kdoc, fused, q_cols, all_kv, head0, keys, values, kv_heads):
    rows = fused.shape[0]
    key_rows = keys.shape[0]
    kv_cols = kv_heads * HEAD_SIZE
    query_group = q_cols // HEAD_SIZE // all_kv
    group_cols = query_group * HEAD_SIZE
    kernel = functools.partial(
        attention_kernel, query_group=query_group, query_blocks=rows // BLK,
        key_offset=key_rows - rows)

    def section(n):
        return pl.BlockSpec((rows, group_cols), lambda g: (0, n * all_kv + head0 + g))

    out_spec = pl.BlockSpec((rows, group_cols), lambda g: (0, g))

    k_spec = pl.BlockSpec((key_rows, HEAD_SIZE), lambda g: (0, head0 + g))
    part_spec = pl.BlockSpec((key_rows, HEAD_SIZE), lambda g: (0, g))
    return pl.pallas_call(
        kernel,
        grid=(kv_heads,),
        in_specs=[
            pl.BlockSpec((rows, 1), lambda g: (0, 0)),
            pl.BlockSpec((1, key_rows), lambda g: (0, 0)),
            section(0), section(1), section(2), k_spec, k_spec,
        ],
        out_specs=[out_spec, part_spec, part_spec],
        out_shape=[
            jax.ShapeDtypeStruct((rows, kv_heads * group_cols), jnp.bfloat16),
            jax.ShapeDtypeStruct((key_rows, kv_cols), jnp.float32),
            jax.ShapeDtypeStruct((key_rows, kv_cols), jnp.float32),
        ],
        compiler_params=pltpu.CompilerParams(
            dimension_semantics=("arbitrary",), vmem_limit_bytes=48 * 1024 * 1024),
    )(qdoc, kdoc, fused, fused, fused, keys, values)


def per_device(query_matrix, key_matrix, value_matrix, fwd_output, output_gradient, block_docs):
    _, q_all = query_matrix.shape
    kv_all = key_matrix.shape[1]
    peers = lax.axis_size("head")
    q_cols, kv_cols = q_all // peers, kv_all // peers
    sections = (query_matrix, output_gradient, fwd_output, key_matrix, value_matrix)
    outgoing = jnp.concatenate(
        [x[:, p * (x.shape[1] // peers):(p + 1) * (x.shape[1] // peers)]
         for p in range(peers) for x in sections], axis=1)
    fused = lax.all_to_all(outgoing, "head", split_axis=1, concat_axis=0, tiled=True)
    window_extent = fused.shape[0]
    key_part = fused[:, 3 * q_cols:3 * q_cols + kv_cols]
    value_part = fused[:, 3 * q_cols + kv_cols:]
    place = lax.axis_index("ctx")
    blocks_here = window_extent // BLK
    own = REACH * window_extent
    skip = own + BLK - DOC_MOST * BLK

    def docs_of(owner):
        docs = lax.dynamic_slice_in_dim(block_docs, jnp.maximum(owner, 0) * blocks_here, blocks_here, 0)
        return jnp.where(owner >= 0, docs, -1)

    key_docs = jnp.concatenate([docs_of(place - distance) for distance in range(REACH, -1, -1)])
    kdoc = jnp.repeat(key_docs, BLK)[skip:][None, :]
    qdoc = jnp.repeat(docs_of(place), BLK)[:, None]
    all_kv = kv_cols // HEAD_SIZE
    per = kv_cols // CHUNKS
    core = lax.axis_index("head")
    ctx_size = lax.axis_size("ctx")

    def half(x, which):
        return lax.dynamic_slice_in_dim(x, which * kv_cols, kv_cols, 1)

    straight = jnp.concatenate([half(key_matrix, core), half(value_matrix, core)], axis=1)
    across = jnp.concatenate([half(key_matrix, 1 - core), half(value_matrix, 1 - core)], axis=1)
    behind_k, behind_v = [], []
    for distance in range(REACH, 0, -1):
        first = max(skip - (REACH - distance) * window_extent, 0)
        if first >= window_extent:
            continue
        mine = shifted(straight, "ctx", distance)
        other = lax.ppermute(across, ("ctx", "head"), [
            (c * peers + p, (c + distance) * peers + (peers - 1 - p))
            for c in range(ctx_size - distance) for p in range(peers)])
        lead = jnp.where(core == 0, mine, other)
        tail = jnp.where(core == 0, other, mine)
        whole = jnp.concatenate([lead, tail], axis=0)[first:]
        behind_k.append(whole[:, :kv_cols])
        behind_v.append(whole[:, kv_cols:])
    keys = jnp.concatenate(behind_k + [key_part], axis=0)
    values = jnp.concatenate(behind_v + [value_part], axis=0)
    q_parts, k_parts, v_parts = [], [], []
    for j in range(CHUNKS):
        query_sum, key_partial, value_partial = local_backward(
            qdoc, kdoc, fused, q_cols, all_kv, j * per // HEAD_SIZE, keys, values,
            per // HEAD_SIZE)

        both = jnp.concatenate([key_partial, value_partial], axis=1)
        total = both[own - skip:]
        for distance in range(1, REACH + 1):
            begin = (REACH - distance) * window_extent
            start = max(begin, skip)
            if start >= begin + window_extent:
                continue
            sent = shifted(
                both[start - skip:begin + window_extent - skip].astype(jnp.bfloat16),
                "ctx", -distance)
            total = total.at[start - begin:].add(sent.astype(jnp.float32))
        q_parts.append(query_sum)
        k_parts.append(total[:, :per].astype(jnp.bfloat16))
        v_parts.append(total[:, per:].astype(jnp.bfloat16))
    finished = jnp.concatenate(q_parts + k_parts + v_parts, axis=1)
    returned = lax.all_to_all(finished, "head", split_axis=0, concat_axis=1, tiled=True)
    width = finished.shape[1]

    def gather(begin, size):
        return jnp.concatenate(
            [returned[:, p * width + begin:p * width + begin + size] for p in range(peers)], axis=1)

    return gather(0, q_cols), gather(q_cols, kv_cols), gather(q_cols + kv_cols, kv_cols)


def solution(mesh):
    return jax.shard_map(
        per_device,
        mesh=mesh,
        in_specs=(
            P(("groups", "ctx", "head"), None),
            P(("groups", "ctx", "head"), None),
            P(("groups", "ctx", "head"), None),
            P(("groups", "ctx", "head"), None),
            P(("groups", "ctx", "head"), None),
            P("groups"),
        ),
        out_specs=(
            P(("groups", "ctx", "head"), None),
            P(("groups", "ctx", "head"), None),
            P(("groups", "ctx", "head"), None),
        ),
        check_vma=False,
    )
```

```python
import functools

import jax
import jax.numpy as jnp
from jax import lax
from jax.experimental import pallas as pl
from jax.experimental.pallas import tpu as pltpu
from jax.sharding import PartitionSpec as P

HEAD_SIZE = 128
BLK = 128
REACH = 2
DOC_MOST = 6
CHUNKS = 2


def shifted(block, axis, distance):
    devices = range(lax.axis_size(axis))
    route = [(i - distance, i) for i in devices if i - distance in devices]
    return lax.ppermute(block, axis, route)


def attention_kernel(qdoc_ref, kdoc_ref, q_ref, do_ref, o_ref, k_ref, v_ref,
                     dq_ref, dk_ref, dv_ref, *, query_group, query_blocks, key_offset):
    scale = HEAD_SIZE ** (-0.5)
    window = DOC_MOST * BLK
    dk_ref[...] = jnp.zeros_like(dk_ref)
    dv_ref[...] = jnp.zeros_like(dv_ref)
    for qb in range(query_blocks):
        rows = pl.ds(qb * BLK, BLK)
        k0 = key_offset + (qb + 1 - DOC_MOST) * BLK
        kwin = k_ref[pl.ds(k0, window), :]
        vwin = v_ref[pl.ds(k0, window), :]
        qs = jnp.concatenate(
            [q_ref[rows, pl.ds(r * HEAD_SIZE, HEAD_SIZE)] for r in range(query_group)], axis=0)
        dos = jnp.concatenate(
            [do_ref[rows, pl.ds(r * HEAD_SIZE, HEAD_SIZE)] for r in range(query_group)], axis=0)
        outs = jnp.concatenate(
            [o_ref[rows, pl.ds(r * HEAD_SIZE, HEAD_SIZE)] for r in range(query_group)], axis=0)
        delta = jnp.sum(dos.astype(jnp.float32) * outs.astype(jnp.float32), axis=1, keepdims=True)
        qd = qdoc_ref[rows, :]
        kd = kdoc_ref[:, pl.ds(k0, window)]
        qpos = lax.broadcasted_iota(jnp.int32, (BLK, window), 0) + (key_offset + qb * BLK)
        kpos = lax.broadcasted_iota(jnp.int32, (BLK, window), 1) + k0
        allowed = (qd == kd) & (kpos <= qpos)
        mask = jnp.concatenate([allowed] * query_group, axis=0)
        scores = scale * lax.dot_general(
            qs, kwin, (((1,), (1,)), ((), ())), preferred_element_type=jnp.float32)
        masked = jnp.where(mask, scores, -1e30)
        top = jnp.max(masked, axis=1, keepdims=True)
        total = jnp.sum(jnp.where(mask, jnp.exp(masked - top), 0.0), axis=1, keepdims=True)
        lse = top + jnp.log(total)
        probs = jnp.where(mask, jnp.exp(masked - lse), 0.0)
        dprob = lax.dot_general(
            dos, vwin, (((1,), (1,)), ((), ())), preferred_element_type=jnp.float32)
        dscore = (probs * (dprob - delta)).astype(jnp.bfloat16)
        dq = scale * jnp.dot(dscore, kwin, preferred_element_type=jnp.float32)
        for r in range(query_group):
            dq_ref[rows, pl.ds(r * HEAD_SIZE, HEAD_SIZE)] = (
                dq[r * BLK:(r + 1) * BLK].astype(dq_ref.dtype))
        dk_ref[pl.ds(k0, window), :] += scale * lax.dot_general(
            dscore, qs, (((0,), (0,)), ((), ())), preferred_element_type=jnp.float32)
        dv_ref[pl.ds(k0, window), :] += lax.dot_general(
            probs.astype(jnp.bfloat16), dos, (((0,), (0,)), ((), ())),
            preferred_element_type=jnp.float32)


def local_backward(qdoc, kdoc, fused, q_cols, all_kv, head0, keys, values):
    rows = fused.shape[0]
    key_rows, kv_cols = keys.shape
    kv_heads = kv_cols // HEAD_SIZE
    query_group = q_cols // HEAD_SIZE // all_kv
    group_cols = query_group * HEAD_SIZE
    kernel = functools.partial(
        attention_kernel, query_group=query_group, query_blocks=rows // BLK,
        key_offset=key_rows - rows)

    def section(n):
        return pl.BlockSpec((rows, group_cols), lambda g: (0, n * all_kv + head0 + g))

    out_spec = pl.BlockSpec((rows, group_cols), lambda g: (0, g))

    k_spec = pl.BlockSpec((key_rows, HEAD_SIZE), lambda g: (0, g))
    return pl.pallas_call(
        kernel,
        grid=(kv_heads,),
        in_specs=[
            pl.BlockSpec((rows, 1), lambda g: (0, 0)),
            pl.BlockSpec((1, key_rows), lambda g: (0, 0)),
            section(0), section(1), section(2), k_spec, k_spec,
        ],
        out_specs=[out_spec, k_spec, k_spec],
        out_shape=[
            jax.ShapeDtypeStruct((rows, kv_heads * group_cols), jnp.bfloat16),
            jax.ShapeDtypeStruct((key_rows, kv_cols), jnp.float32),
            jax.ShapeDtypeStruct((key_rows, kv_cols), jnp.float32),
        ],
        compiler_params=pltpu.CompilerParams(
            dimension_semantics=("arbitrary",), vmem_limit_bytes=48 * 1024 * 1024),
    )(qdoc, kdoc, fused, fused, fused, keys, values)


def per_device(query_matrix, key_matrix, value_matrix, fwd_output, output_gradient, block_docs):
    _, q_all = query_matrix.shape
    kv_all = key_matrix.shape[1]
    peers = lax.axis_size("head")
    q_cols, kv_cols = q_all // peers, kv_all // peers
    sections = (query_matrix, output_gradient, fwd_output, key_matrix, value_matrix)
    outgoing = jnp.concatenate(
        [x[:, p * (x.shape[1] // peers):(p + 1) * (x.shape[1] // peers)]
         for p in range(peers) for x in sections], axis=1)
    fused = lax.all_to_all(outgoing, "head", split_axis=1, concat_axis=0, tiled=True)
    window_extent = fused.shape[0]
    key_part = fused[:, 3 * q_cols:3 * q_cols + kv_cols]
    value_part = fused[:, 3 * q_cols + kv_cols:]
    place = lax.axis_index("ctx")
    blocks_here = window_extent // BLK
    own = REACH * window_extent
    skip = own + BLK - DOC_MOST * BLK

    def docs_of(owner):
        docs = lax.dynamic_slice_in_dim(block_docs, jnp.maximum(owner, 0) * blocks_here, blocks_here, 0)
        return jnp.where(owner >= 0, docs, -1)

    key_docs = jnp.concatenate([docs_of(place - distance) for distance in range(REACH, -1, -1)])
    kdoc = jnp.repeat(key_docs, BLK)[skip:][None, :]
    qdoc = jnp.repeat(docs_of(place), BLK)[:, None]
    all_kv = kv_cols // HEAD_SIZE
    per = kv_cols // CHUNKS
    q_parts, k_parts, v_parts = [], [], []
    for j in range(CHUNKS):
        key_here = key_part[:, j * per:(j + 1) * per]
        value_here = value_part[:, j * per:(j + 1) * per]
        pair = jnp.concatenate([key_here, value_here], axis=1)
        behind = []
        for distance in range(REACH, 0, -1):
            first = max(skip - (REACH - distance) * window_extent, 0)
            if first < window_extent:
                behind.append(shifted(pair[first:], "ctx", distance))
        keys = jnp.concatenate([b[:, :per] for b in behind] + [key_here], axis=0)
        values = jnp.concatenate([b[:, per:] for b in behind] + [value_here], axis=0)

        query_sum, key_partial, value_partial = local_backward(
            qdoc, kdoc, fused, q_cols, all_kv, j * per // HEAD_SIZE, keys, values)

        both = jnp.concatenate([key_partial, value_partial], axis=1)
        total = both[own - skip:]
        for distance in range(1, REACH + 1):
            begin = (REACH - distance) * window_extent
            start = max(begin, skip)
            if start >= begin + window_extent:
                continue
            sent = shifted(
                both[start - skip:begin + window_extent - skip].astype(jnp.bfloat16),
                "ctx", -distance)
            total = total.at[start - begin:].add(sent.astype(jnp.float32))
        q_parts.append(query_sum)
        k_parts.append(total[:, :per].astype(jnp.bfloat16))
        v_parts.append(total[:, per:].astype(jnp.bfloat16))
    query_back = lax.all_to_all(
        jnp.concatenate(q_parts, axis=1), "head", split_axis=0, concat_axis=1, tiled=True)
    finished = jnp.concatenate(k_parts + v_parts, axis=1)
    returned = lax.all_to_all(finished, "head", split_axis=0, concat_axis=1, tiled=True)
    width = finished.shape[1]

    def gather(begin, size):
        return jnp.concatenate(
            [returned[:, p * width + begin:p * width + begin + size] for p in range(peers)], axis=1)

    return query_back, gather(0, kv_cols), gather(kv_cols, kv_cols)


def solution(mesh):
    return jax.shard_map(
        per_device,
        mesh=mesh,
        in_specs=(
            P(("groups", "ctx", "head"), None),
            P(("groups", "ctx", "head"), None),
            P(("groups", "ctx", "head"), None),
            P(("groups", "ctx", "head"), None),
            P(("groups", "ctx", "head"), None),
            P("groups"),
        ),
        out_specs=(
            P(("groups", "ctx", "head"), None),
            P(("groups", "ctx", "head"), None),
            P(("groups", "ctx", "head"), None),
        ),
        check_vma=False,
    )
```

```python
import functools

import jax
import jax.numpy as jnp
from jax import lax
from jax.experimental import pallas as pl
from jax.experimental.pallas import tpu as pltpu
from jax.sharding import PartitionSpec as P

HEAD_SIZE = 128
BLK = 128
REACH = 2
DOC_MOST = 6
CHUNKS = 4
ENTRY_CHUNKS = 2


def shifted(block, axis, distance):
    devices = range(lax.axis_size(axis))
    route = [(i - distance, i) for i in devices if i - distance in devices]
    return lax.ppermute(block, axis, route)


def attention_kernel(qdoc_ref, kdoc_ref, q_ref, do_ref, o_ref, k_ref, v_ref,
                     dq_ref, dk_ref, dv_ref, *, query_group, query_blocks, key_offset):
    scale = HEAD_SIZE ** (-0.5)
    window = DOC_MOST * BLK
    dk_ref[...] = jnp.zeros_like(dk_ref)
    dv_ref[...] = jnp.zeros_like(dv_ref)
    for qb in range(query_blocks):
        rows = pl.ds(qb * BLK, BLK)
        k0 = key_offset + (qb + 1 - DOC_MOST) * BLK
        kwin = k_ref[pl.ds(k0, window), :]
        vwin = v_ref[pl.ds(k0, window), :]
        qs = jnp.concatenate(
            [q_ref[rows, pl.ds(r * HEAD_SIZE, HEAD_SIZE)] for r in range(query_group)], axis=0)
        dos = jnp.concatenate(
            [do_ref[rows, pl.ds(r * HEAD_SIZE, HEAD_SIZE)] for r in range(query_group)], axis=0)
        outs = jnp.concatenate(
            [o_ref[rows, pl.ds(r * HEAD_SIZE, HEAD_SIZE)] for r in range(query_group)], axis=0)
        delta = jnp.sum(dos.astype(jnp.float32) * outs.astype(jnp.float32), axis=1, keepdims=True)
        qd = qdoc_ref[rows, :]
        kd = kdoc_ref[:, pl.ds(k0, window)]
        qpos = lax.broadcasted_iota(jnp.int32, (BLK, window), 0) + (key_offset + qb * BLK)
        kpos = lax.broadcasted_iota(jnp.int32, (BLK, window), 1) + k0
        allowed = (qd == kd) & (kpos <= qpos)
        mask = jnp.concatenate([allowed] * query_group, axis=0)
        scores = scale * lax.dot_general(
            qs, kwin, (((1,), (1,)), ((), ())), preferred_element_type=jnp.float32)
        masked = jnp.where(mask, scores, -1e30)
        top = jnp.max(masked, axis=1, keepdims=True)
        total = jnp.sum(jnp.exp(masked - top), axis=1, keepdims=True)
        lse = top + jnp.log(total)
        probs = jnp.exp(masked - lse)
        dprob = lax.dot_general(
            dos, vwin, (((1,), (1,)), ((), ())), preferred_element_type=jnp.float32)
        dscore = (probs * (dprob - delta)).astype(jnp.bfloat16)
        dq = scale * jnp.dot(dscore, kwin, preferred_element_type=jnp.float32)
        for r in range(query_group):
            dq_ref[rows, pl.ds(r * HEAD_SIZE, HEAD_SIZE)] = (
                dq[r * BLK:(r + 1) * BLK].astype(dq_ref.dtype))
        dk_ref[pl.ds(k0, window), :] += scale * lax.dot_general(
            dscore, qs, (((0,), (0,)), ((), ())), preferred_element_type=jnp.float32)
        dv_ref[pl.ds(k0, window), :] += lax.dot_general(
            probs.astype(jnp.bfloat16), dos, (((0,), (0,)), ((), ())),
            preferred_element_type=jnp.float32)


def local_backward(qdoc, kdoc, fused, q_cols, all_kv, head0, keys, values, key_head0, kv_heads):
    rows = fused.shape[0]
    key_rows = keys.shape[0]
    kv_cols = kv_heads * HEAD_SIZE
    query_group = q_cols // HEAD_SIZE // all_kv
    group_cols = query_group * HEAD_SIZE
    kernel = functools.partial(
        attention_kernel, query_group=query_group, query_blocks=rows // BLK,
        key_offset=key_rows - rows)

    def section(n):
        return pl.BlockSpec((rows, group_cols), lambda g: (0, n * all_kv + head0 + g))

    out_spec = pl.BlockSpec((rows, group_cols), lambda g: (0, g))

    k_spec = pl.BlockSpec((key_rows, HEAD_SIZE), lambda g: (0, key_head0 + g))
    part_spec = pl.BlockSpec((key_rows, HEAD_SIZE), lambda g: (0, g))
    return pl.pallas_call(
        kernel,
        grid=(kv_heads,),
        in_specs=[
            pl.BlockSpec((rows, 1), lambda g: (0, 0)),
            pl.BlockSpec((1, key_rows), lambda g: (0, 0)),
            section(0), section(1), section(2), k_spec, k_spec,
        ],
        out_specs=[out_spec, part_spec, part_spec],
        out_shape=[
            jax.ShapeDtypeStruct((rows, kv_heads * group_cols), jnp.bfloat16),
            jax.ShapeDtypeStruct((key_rows, kv_cols), jnp.float32),
            jax.ShapeDtypeStruct((key_rows, kv_cols), jnp.float32),
        ],
        compiler_params=pltpu.CompilerParams(
            dimension_semantics=("arbitrary",), vmem_limit_bytes=48 * 1024 * 1024),
    )(qdoc, kdoc, fused, fused, fused, keys, values)


def per_device(query_matrix, key_matrix, value_matrix, fwd_output, output_gradient, block_docs):
    _, q_all = query_matrix.shape
    kv_all = key_matrix.shape[1]
    peers = lax.axis_size("head")
    q_cols, kv_cols = q_all // peers, kv_all // peers
    sections = (query_matrix, output_gradient, fwd_output, key_matrix, value_matrix)
    outgoing = jnp.concatenate(
        [x[:, p * (x.shape[1] // peers):(p + 1) * (x.shape[1] // peers)]
         for p in range(peers) for x in sections], axis=1)
    fused = lax.all_to_all(outgoing, "head", split_axis=1, concat_axis=0, tiled=True)
    window_extent = fused.shape[0]
    key_part = fused[:, 3 * q_cols:3 * q_cols + kv_cols]
    value_part = fused[:, 3 * q_cols + kv_cols:]
    place = lax.axis_index("ctx")
    blocks_here = window_extent // BLK
    own = REACH * window_extent
    skip = own + BLK - DOC_MOST * BLK

    def docs_of(owner):
        docs = lax.dynamic_slice_in_dim(block_docs, jnp.maximum(owner, 0) * blocks_here, blocks_here, 0)
        return jnp.where(owner >= 0, docs, -1)

    key_docs = jnp.concatenate([docs_of(place - distance) for distance in range(REACH, -1, -1)])
    kdoc = jnp.repeat(key_docs, BLK)[skip:][None, :]
    qdoc = jnp.repeat(docs_of(place), BLK)[:, None]
    all_kv = kv_cols // HEAD_SIZE
    per = kv_cols // CHUNKS
    entry_per = kv_cols // ENTRY_CHUNKS
    entries = []
    for e in range(ENTRY_CHUNKS):
        key_here = key_part[:, e * entry_per:(e + 1) * entry_per]
        value_here = value_part[:, e * entry_per:(e + 1) * entry_per]
        pair = jnp.concatenate([key_here, value_here], axis=1)
        behind = []
        for distance in range(REACH, 0, -1):
            first = max(skip - (REACH - distance) * window_extent, 0)
            if first < window_extent:
                behind.append(shifted(pair[first:], "ctx", distance))
        keys = jnp.concatenate([b[:, :entry_per] for b in behind] + [key_here], axis=0)
        values = jnp.concatenate([b[:, entry_per:] for b in behind] + [value_here], axis=0)
        entries.append((keys, values))
    q_parts, k_parts, v_parts = [], [], []
    for j in range(CHUNKS):
        keys, values = entries[j * per // entry_per]
        query_sum, key_partial, value_partial = local_backward(
            qdoc, kdoc, fused, q_cols, all_kv, j * per // HEAD_SIZE, keys, values,
            (j * per % entry_per) // HEAD_SIZE, per // HEAD_SIZE)

        both = jnp.concatenate([key_partial, value_partial], axis=1)
        total = both[own - skip:]
        for distance in range(1, REACH + 1):
            begin = (REACH - distance) * window_extent
            start = max(begin, skip)
            if start >= begin + window_extent:
                continue
            sent = shifted(
                both[start - skip:begin + window_extent - skip].astype(jnp.bfloat16),
                "ctx", -distance)
            total = total.at[start - begin:].add(sent.astype(jnp.float32))
        q_parts.append(query_sum)
        k_parts.append(total[:, :per].astype(jnp.bfloat16))
        v_parts.append(total[:, per:].astype(jnp.bfloat16))
    finished = jnp.concatenate(q_parts + k_parts + v_parts, axis=1)
    returned = lax.all_to_all(finished, "head", split_axis=0, concat_axis=1, tiled=True)
    width = finished.shape[1]

    def gather(begin, size):
        return jnp.concatenate(
            [returned[:, p * width + begin:p * width + begin + size] for p in range(peers)], axis=1)

    return gather(0, q_cols), gather(q_cols, kv_cols), gather(q_cols + kv_cols, kv_cols)


def solution(mesh):
    return jax.shard_map(
        per_device,
        mesh=mesh,
        in_specs=(
            P(("groups", "ctx", "head"), None),
            P(("groups", "ctx", "head"), None),
            P(("groups", "ctx", "head"), None),
            P(("groups", "ctx", "head"), None),
            P(("groups", "ctx", "head"), None),
            P("groups"),
        ),
        out_specs=(
            P(("groups", "ctx", "head"), None),
            P(("groups", "ctx", "head"), None),
            P(("groups", "ctx", "head"), None),
        ),
        check_vma=False,
    )
```

```python
import functools

import jax
import jax.numpy as jnp
from jax import lax
from jax.experimental import pallas as pl
from jax.experimental.pallas import tpu as pltpu
from jax.sharding import PartitionSpec as P

HEAD_SIZE = 128
BLK = 128
REACH = 2
DOC_MOST = 6
CHUNKS = 2


def shifted(block, axis, distance):
    devices = range(lax.axis_size(axis))
    route = [(i - distance, i) for i in devices if i - distance in devices]
    return lax.ppermute(block, axis, route)


def attention_kernel(qdoc_ref, kdoc_ref, q_ref, do_ref, d_ref, k_ref, v_ref,
                     dq_ref, dk_ref, dv_ref, *, query_group, query_blocks, key_offset):
    scale = HEAD_SIZE ** (-0.5)
    window = DOC_MOST * BLK
    dk_ref[...] = jnp.zeros_like(dk_ref)
    dv_ref[...] = jnp.zeros_like(dv_ref)
    for qb in range(query_blocks):
        rows = pl.ds(qb * BLK, BLK)
        k0 = key_offset + (qb + 1 - DOC_MOST) * BLK
        kwin = k_ref[pl.ds(k0, window), :]
        vwin = v_ref[pl.ds(k0, window), :]
        qs = jnp.concatenate(
            [q_ref[rows, pl.ds(r * HEAD_SIZE, HEAD_SIZE)] for r in range(query_group)], axis=0)
        dos = jnp.concatenate(
            [do_ref[rows, pl.ds(r * HEAD_SIZE, HEAD_SIZE)] for r in range(query_group)], axis=0)
        pieces = d_ref[rows, :].astype(jnp.float32)
        delta = jnp.concatenate(
            [pieces[:, r:r + 1] + pieces[:, query_group + r:query_group + r + 1]
             + pieces[:, 2 * query_group + r:2 * query_group + r + 1]
             for r in range(query_group)], axis=0)
        qd = qdoc_ref[rows, :]
        kd = kdoc_ref[:, pl.ds(k0, window)]
        qpos = lax.broadcasted_iota(jnp.int32, (BLK, window), 0) + (key_offset + qb * BLK)
        kpos = lax.broadcasted_iota(jnp.int32, (BLK, window), 1) + k0
        allowed = (qd == kd) & (kpos <= qpos)
        mask = jnp.concatenate([allowed] * query_group, axis=0)
        scores = scale * lax.dot_general(
            qs, kwin, (((1,), (1,)), ((), ())), preferred_element_type=jnp.float32)
        masked = jnp.where(mask, scores, -1e30)
        top = jnp.max(masked, axis=1, keepdims=True)
        total = jnp.sum(jnp.exp(masked - top), axis=1, keepdims=True)
        lse = top + jnp.log(total)
        probs = jnp.exp(masked - lse)
        dprob = lax.dot_general(
            dos, vwin, (((1,), (1,)), ((), ())), preferred_element_type=jnp.float32)
        dscore = (probs * (dprob - delta)).astype(jnp.bfloat16)
        dq = scale * jnp.dot(dscore, kwin, preferred_element_type=jnp.float32)
        for r in range(query_group):
            dq_ref[rows, pl.ds(r * HEAD_SIZE, HEAD_SIZE)] = (
                dq[r * BLK:(r + 1) * BLK].astype(dq_ref.dtype))
        dk_ref[pl.ds(k0, window), :] += scale * lax.dot_general(
            dscore, qs, (((0,), (0,)), ((), ())), preferred_element_type=jnp.float32)
        dv_ref[pl.ds(k0, window), :] += lax.dot_general(
            probs.astype(jnp.bfloat16), dos, (((0,), (0,)), ((), ())),
            preferred_element_type=jnp.float32)


def local_backward(qdoc, kdoc, fused, q_cols, all_kv, head0, keys, values):
    rows = fused.shape[0]
    key_rows, kv_cols = keys.shape
    kv_heads = kv_cols // HEAD_SIZE
    query_group = q_cols // HEAD_SIZE // all_kv
    group_cols = query_group * HEAD_SIZE
    kernel = functools.partial(
        attention_kernel, query_group=query_group, query_blocks=rows // BLK,
        key_offset=key_rows - rows)

    def section(n):
        return pl.BlockSpec((rows, group_cols), lambda g: (0, n * all_kv + head0 + g))

    out_spec = pl.BlockSpec((rows, group_cols), lambda g: (0, g))

    k_spec = pl.BlockSpec((key_rows, HEAD_SIZE), lambda g: (0, g))
    return pl.pallas_call(
        kernel,
        grid=(kv_heads,),
        in_specs=[
            pl.BlockSpec((rows, 1), lambda g: (0, 0)),
            pl.BlockSpec((1, key_rows), lambda g: (0, 0)),
            section(0), section(1),
            pl.BlockSpec((rows, HEAD_SIZE),
                         lambda g: (0, 2 * q_cols // HEAD_SIZE + 2 * all_kv + head0 + g)),
            k_spec, k_spec,
        ],
        out_specs=[out_spec, k_spec, k_spec],
        out_shape=[
            jax.ShapeDtypeStruct((rows, kv_heads * group_cols), jnp.bfloat16),
            jax.ShapeDtypeStruct((key_rows, kv_cols), jnp.float32),
            jax.ShapeDtypeStruct((key_rows, kv_cols), jnp.float32),
        ],
        compiler_params=pltpu.CompilerParams(
            dimension_semantics=("arbitrary",), vmem_limit_bytes=48 * 1024 * 1024),
    )(qdoc, kdoc, fused, fused, fused, keys, values)


def per_device(query_matrix, key_matrix, value_matrix, fwd_output, output_gradient, block_docs):
    tokens, q_all = query_matrix.shape
    kv_all = key_matrix.shape[1]
    peers = lax.axis_size("head")
    q_cols, kv_cols = q_all // peers, kv_all // peers
    all_heads = q_all // HEAD_SIZE
    all_kv = kv_cols // HEAD_SIZE
    group = all_heads // peers // all_kv
    delta_here = jnp.sum(
        output_gradient.reshape(tokens, all_heads, HEAD_SIZE).astype(jnp.float32)
        * fwd_output.reshape(tokens, all_heads, HEAD_SIZE).astype(jnp.float32),
        axis=2,
    )
    hi = lax.reduce_precision(delta_here, exponent_bits=8, mantissa_bits=7)
    rest = delta_here - hi
    mid = lax.reduce_precision(rest, exponent_bits=8, mantissa_bits=7)
    pieces = jnp.stack([hi, mid, rest - mid]).astype(jnp.bfloat16)
    pieces = pieces.reshape(3, tokens, peers, all_kv, group).transpose(1, 2, 3, 0, 4)
    pieces = jnp.pad(pieces.reshape(tokens, peers, all_kv, 3 * group),
                     ((0, 0), (0, 0), (0, 0), (0, HEAD_SIZE - 3 * group)))
    pieces = pieces.reshape(tokens, peers * all_kv * HEAD_SIZE)
    sections = (query_matrix, output_gradient, key_matrix, value_matrix, pieces)
    outgoing = jnp.concatenate(
        [x[:, p * (x.shape[1] // peers):(p + 1) * (x.shape[1] // peers)]
         for p in range(peers) for x in sections], axis=1)
    fused = lax.all_to_all(outgoing, "head", split_axis=1, concat_axis=0, tiled=True)
    window_extent = fused.shape[0]
    key_part = fused[:, 2 * q_cols:2 * q_cols + kv_cols]
    value_part = fused[:, 2 * q_cols + kv_cols:2 * q_cols + 2 * kv_cols]
    place = lax.axis_index("ctx")
    blocks_here = window_extent // BLK
    own = REACH * window_extent
    skip = own + BLK - DOC_MOST * BLK

    def docs_of(owner):
        docs = lax.dynamic_slice_in_dim(block_docs, jnp.maximum(owner, 0) * blocks_here, blocks_here, 0)
        return jnp.where(owner >= 0, docs, -1)

    key_docs = jnp.concatenate([docs_of(place - distance) for distance in range(REACH, -1, -1)])
    kdoc = jnp.repeat(key_docs, BLK)[skip:][None, :]
    qdoc = jnp.repeat(docs_of(place), BLK)[:, None]
    per = kv_cols // CHUNKS
    q_parts, k_parts, v_parts = [], [], []
    for j in range(CHUNKS):
        key_here = key_part[:, j * per:(j + 1) * per]
        value_here = value_part[:, j * per:(j + 1) * per]
        pair = jnp.concatenate([key_here, value_here], axis=1)
        behind = []
        for distance in range(REACH, 0, -1):
            first = max(skip - (REACH - distance) * window_extent, 0)
            if first < window_extent:
                behind.append(shifted(pair[first:], "ctx", distance))
        keys = jnp.concatenate([b[:, :per] for b in behind] + [key_here], axis=0)
        values = jnp.concatenate([b[:, per:] for b in behind] + [value_here], axis=0)

        query_sum, key_partial, value_partial = local_backward(
            qdoc, kdoc, fused, q_cols, all_kv, j * per // HEAD_SIZE, keys, values)

        both = jnp.concatenate([key_partial, value_partial], axis=1)
        total = both[own - skip:]
        for distance in range(1, REACH + 1):
            begin = (REACH - distance) * window_extent
            start = max(begin, skip)
            if start >= begin + window_extent:
                continue
            sent = shifted(
                both[start - skip:begin + window_extent - skip].astype(jnp.bfloat16),
                "ctx", -distance)
            total = total.at[start - begin:].add(sent.astype(jnp.float32))
        q_parts.append(query_sum)
        k_parts.append(total[:, :per].astype(jnp.bfloat16))
        v_parts.append(total[:, per:].astype(jnp.bfloat16))
    finished = jnp.concatenate(q_parts + k_parts + v_parts, axis=1)
    returned = lax.all_to_all(finished, "head", split_axis=0, concat_axis=1, tiled=True)
    width = finished.shape[1]

    def gather(begin, size):
        return jnp.concatenate(
            [returned[:, p * width + begin:p * width + begin + size] for p in range(peers)], axis=1)

    return gather(0, q_cols), gather(q_cols, kv_cols), gather(q_cols + kv_cols, kv_cols)


def solution(mesh):
    return jax.shard_map(
        per_device,
        mesh=mesh,
        in_specs=(
            P(("groups", "ctx", "head"), None),
            P(("groups", "ctx", "head"), None),
            P(("groups", "ctx", "head"), None),
            P(("groups", "ctx", "head"), None),
            P(("groups", "ctx", "head"), None),
            P("groups"),
        ),
        out_specs=(
            P(("groups", "ctx", "head"), None),
            P(("groups", "ctx", "head"), None),
            P(("groups", "ctx", "head"), None),
        ),
        check_vma=False,
    )
```

```python
import functools

import jax
import jax.numpy as jnp
from jax import lax
from jax.experimental import pallas as pl
from jax.experimental.pallas import tpu as pltpu
from jax.sharding import PartitionSpec as P

HEAD_SIZE = 128
BLK = 128
REACH = 2
DOC_MOST = 6
CHUNKS = 2
SHARES = (3, 1)


def shifted(block, axis, distance):
    devices = range(lax.axis_size(axis))
    route = [(i - distance, i) for i in devices if i - distance in devices]
    return lax.ppermute(block, axis, route)


def attention_kernel(qdoc_ref, kdoc_ref, q_ref, do_ref, o_ref, k_ref, v_ref,
                     dq_ref, dk_ref, dv_ref, *, query_group, query_blocks, key_offset):
    scale = HEAD_SIZE ** (-0.5)
    window = DOC_MOST * BLK
    dk_ref[...] = jnp.zeros_like(dk_ref)
    dv_ref[...] = jnp.zeros_like(dv_ref)
    for qb in range(query_blocks):
        rows = pl.ds(qb * BLK, BLK)
        k0 = key_offset + (qb + 1 - DOC_MOST) * BLK
        kwin = k_ref[pl.ds(k0, window), :]
        vwin = v_ref[pl.ds(k0, window), :]
        qs = jnp.concatenate(
            [q_ref[rows, pl.ds(r * HEAD_SIZE, HEAD_SIZE)] for r in range(query_group)], axis=0)
        dos = jnp.concatenate(
            [do_ref[rows, pl.ds(r * HEAD_SIZE, HEAD_SIZE)] for r in range(query_group)], axis=0)
        outs = jnp.concatenate(
            [o_ref[rows, pl.ds(r * HEAD_SIZE, HEAD_SIZE)] for r in range(query_group)], axis=0)
        delta = jnp.sum(dos.astype(jnp.float32) * outs.astype(jnp.float32), axis=1, keepdims=True)
        qd = qdoc_ref[rows, :]
        kd = kdoc_ref[:, pl.ds(k0, window)]
        qpos = lax.broadcasted_iota(jnp.int32, (BLK, window), 0) + (key_offset + qb * BLK)
        kpos = lax.broadcasted_iota(jnp.int32, (BLK, window), 1) + k0
        allowed = (qd == kd) & (kpos <= qpos)
        mask = jnp.concatenate([allowed] * query_group, axis=0)
        scores = scale * lax.dot_general(
            qs, kwin, (((1,), (1,)), ((), ())), preferred_element_type=jnp.float32)
        masked = jnp.where(mask, scores, -1e30)
        top = jnp.max(masked, axis=1, keepdims=True)
        total = jnp.sum(jnp.exp(masked - top), axis=1, keepdims=True)
        lse = top + jnp.log(total)
        probs = jnp.exp(masked - lse)
        dprob = lax.dot_general(
            dos, vwin, (((1,), (1,)), ((), ())), preferred_element_type=jnp.float32)
        dscore = (probs * (dprob - delta)).astype(jnp.bfloat16)
        dq = scale * jnp.dot(dscore, kwin, preferred_element_type=jnp.float32)
        for r in range(query_group):
            dq_ref[rows, pl.ds(r * HEAD_SIZE, HEAD_SIZE)] = (
                dq[r * BLK:(r + 1) * BLK].astype(dq_ref.dtype))
        dk_ref[pl.ds(k0, window), :] += scale * lax.dot_general(
            dscore, qs, (((0,), (0,)), ((), ())), preferred_element_type=jnp.float32)
        dv_ref[pl.ds(k0, window), :] += lax.dot_general(
            probs.astype(jnp.bfloat16), dos, (((0,), (0,)), ((), ())),
            preferred_element_type=jnp.float32)


def local_backward(qdoc, kdoc, fused, q_cols, all_kv, head0, keys, values):
    rows = fused.shape[0]
    key_rows, kv_cols = keys.shape
    kv_heads = kv_cols // HEAD_SIZE
    query_group = q_cols // HEAD_SIZE // all_kv
    group_cols = query_group * HEAD_SIZE
    kernel = functools.partial(
        attention_kernel, query_group=query_group, query_blocks=rows // BLK,
        key_offset=key_rows - rows)

    def section(n):
        return pl.BlockSpec((rows, group_cols), lambda g: (0, n * all_kv + head0 + g))

    out_spec = pl.BlockSpec((rows, group_cols), lambda g: (0, g))

    k_spec = pl.BlockSpec((key_rows, HEAD_SIZE), lambda g: (0, g))
    return pl.pallas_call(
        kernel,
        grid=(kv_heads,),
        in_specs=[
            pl.BlockSpec((rows, 1), lambda g: (0, 0)),
            pl.BlockSpec((1, key_rows), lambda g: (0, 0)),
            section(0), section(1), section(2), k_spec, k_spec,
        ],
        out_specs=[out_spec, k_spec, k_spec],
        out_shape=[
            jax.ShapeDtypeStruct((rows, kv_heads * group_cols), jnp.bfloat16),
            jax.ShapeDtypeStruct((key_rows, kv_cols), jnp.float32),
            jax.ShapeDtypeStruct((key_rows, kv_cols), jnp.float32),
        ],
        compiler_params=pltpu.CompilerParams(
            dimension_semantics=("arbitrary",), vmem_limit_bytes=48 * 1024 * 1024),
    )(qdoc, kdoc, fused, fused, fused, keys, values)


def per_device(query_matrix, key_matrix, value_matrix, fwd_output, output_gradient, block_docs):
    _, q_all = query_matrix.shape
    kv_all = key_matrix.shape[1]
    peers = lax.axis_size("head")
    q_cols, kv_cols = q_all // peers, kv_all // peers
    sections = (query_matrix, output_gradient, fwd_output, key_matrix, value_matrix)
    outgoing = jnp.concatenate(
        [x[:, p * (x.shape[1] // peers):(p + 1) * (x.shape[1] // peers)]
         for p in range(peers) for x in sections], axis=1)
    fused = lax.all_to_all(outgoing, "head", split_axis=1, concat_axis=0, tiled=True)
    window_extent = fused.shape[0]
    key_part = fused[:, 3 * q_cols:3 * q_cols + kv_cols]
    value_part = fused[:, 3 * q_cols + kv_cols:]
    place = lax.axis_index("ctx")
    blocks_here = window_extent // BLK
    own = REACH * window_extent
    skip = own + BLK - DOC_MOST * BLK

    def docs_of(owner):
        docs = lax.dynamic_slice_in_dim(block_docs, jnp.maximum(owner, 0) * blocks_here, blocks_here, 0)
        return jnp.where(owner >= 0, docs, -1)

    key_docs = jnp.concatenate([docs_of(place - distance) for distance in range(REACH, -1, -1)])
    kdoc = jnp.repeat(key_docs, BLK)[skip:][None, :]
    qdoc = jnp.repeat(docs_of(place), BLK)[:, None]
    all_kv = kv_cols // HEAD_SIZE
    unit = kv_cols // sum(SHARES)
    q_parts, k_parts, v_parts = [], [], []
    for j in range(CHUNKS):
        lo = sum(SHARES[:j]) * unit
        per = SHARES[j] * unit
        key_here = key_part[:, lo:lo + per]
        value_here = value_part[:, lo:lo + per]
        pair = jnp.concatenate([key_here, value_here], axis=1)
        behind = []
        for distance in range(REACH, 0, -1):
            first = max(skip - (REACH - distance) * window_extent, 0)
            if first < window_extent:
                behind.append(shifted(pair[first:], "ctx", distance))
        keys = jnp.concatenate([b[:, :per] for b in behind] + [key_here], axis=0)
        values = jnp.concatenate([b[:, per:] for b in behind] + [value_here], axis=0)

        query_sum, key_partial, value_partial = local_backward(
            qdoc, kdoc, fused, q_cols, all_kv, lo // HEAD_SIZE, keys, values)

        both = jnp.concatenate([key_partial, value_partial], axis=1)
        total = both[own - skip:]
        for distance in range(1, REACH + 1):
            begin = (REACH - distance) * window_extent
            start = max(begin, skip)
            if start >= begin + window_extent:
                continue
            sent = shifted(
                both[start - skip:begin + window_extent - skip].astype(jnp.bfloat16),
                "ctx", -distance)
            total = total.at[start - begin:].add(sent.astype(jnp.float32))
        q_parts.append(query_sum)
        k_parts.append(total[:, :per].astype(jnp.bfloat16))
        v_parts.append(total[:, per:].astype(jnp.bfloat16))
    finished = jnp.concatenate(q_parts + k_parts + v_parts, axis=1)
    returned = lax.all_to_all(finished, "head", split_axis=0, concat_axis=1, tiled=True)
    width = finished.shape[1]

    def gather(begin, size):
        return jnp.concatenate(
            [returned[:, p * width + begin:p * width + begin + size] for p in range(peers)], axis=1)

    return gather(0, q_cols), gather(q_cols, kv_cols), gather(q_cols + kv_cols, kv_cols)


def solution(mesh):
    return jax.shard_map(
        per_device,
        mesh=mesh,
        in_specs=(
            P(("groups", "ctx", "head"), None),
            P(("groups", "ctx", "head"), None),
            P(("groups", "ctx", "head"), None),
            P(("groups", "ctx", "head"), None),
            P(("groups", "ctx", "head"), None),
            P("groups"),
        ),
        out_specs=(
            P(("groups", "ctx", "head"), None),
            P(("groups", "ctx", "head"), None),
            P(("groups", "ctx", "head"), None),
        ),
        check_vma=False,
    )
```

```python
import functools

import jax
import jax.numpy as jnp
from jax import lax
from jax.experimental import pallas as pl
from jax.experimental.pallas import tpu as pltpu
from jax.sharding import PartitionSpec as P

HEAD_SIZE = 128
BLK = 128
REACH = 2
DOC_MOST = 6
CHUNKS = 2


def shifted(block, axis, distance):
    devices = range(lax.axis_size(axis))
    route = [(i - distance, i) for i in devices if i - distance in devices]
    return lax.ppermute(block, axis, route)


def attention_kernel(qdoc_ref, kdoc_ref, q_ref, do_ref, o_ref, k_ref, v_ref,
                     dq_ref, dk_ref, dv_ref, *, query_group, query_blocks, key_offset):
    scale = HEAD_SIZE ** (-0.5)
    window = DOC_MOST * BLK
    dk_ref[...] = jnp.zeros_like(dk_ref)
    dv_ref[...] = jnp.zeros_like(dv_ref)
    for qb in range(query_blocks):
        rows = pl.ds(qb * BLK, BLK)
        k0 = key_offset + (qb + 1 - DOC_MOST) * BLK
        kwin = k_ref[pl.ds(k0, window), :]
        vwin = v_ref[pl.ds(k0, window), :]
        qs = jnp.concatenate(
            [q_ref[rows, pl.ds(r * HEAD_SIZE, HEAD_SIZE)] for r in range(query_group)], axis=0)
        dos = jnp.concatenate(
            [do_ref[rows, pl.ds(r * HEAD_SIZE, HEAD_SIZE)] for r in range(query_group)], axis=0)
        outs = jnp.concatenate(
            [o_ref[rows, pl.ds(r * HEAD_SIZE, HEAD_SIZE)] for r in range(query_group)], axis=0)
        delta = jnp.sum(dos.astype(jnp.float32) * outs.astype(jnp.float32), axis=1, keepdims=True)
        qd = qdoc_ref[rows, :]
        kd = kdoc_ref[:, pl.ds(k0, window)]
        qpos = lax.broadcasted_iota(jnp.int32, (BLK, window), 0) + (key_offset + qb * BLK)
        kpos = lax.broadcasted_iota(jnp.int32, (BLK, window), 1) + k0
        allowed = (qd == kd) & (kpos <= qpos)
        mask = jnp.concatenate([allowed] * query_group, axis=0)
        scores = scale * lax.dot_general(
            qs, kwin, (((1,), (1,)), ((), ())), preferred_element_type=jnp.float32)
        masked = jnp.where(mask, scores, -1e30)
        top = jnp.max(masked, axis=1, keepdims=True)
        total = jnp.sum(jnp.exp(masked - top), axis=1, keepdims=True)
        lse = top + jnp.log(total)
        probs = jnp.exp(masked - lse)
        dprob = lax.dot_general(
            dos, vwin, (((1,), (1,)), ((), ())), preferred_element_type=jnp.float32)
        dscore = (probs * (dprob - delta)).astype(jnp.bfloat16)
        dq = scale * jnp.dot(dscore, kwin, preferred_element_type=jnp.float32)
        for r in range(query_group):
            dq_ref[rows, pl.ds(r * HEAD_SIZE, HEAD_SIZE)] = (
                dq[r * BLK:(r + 1) * BLK].astype(dq_ref.dtype))
        dk_ref[pl.ds(k0, window), :] += scale * lax.dot_general(
            dscore, qs, (((0,), (0,)), ((), ())), preferred_element_type=jnp.float32)
        dv_ref[pl.ds(k0, window), :] += lax.dot_general(
            probs.astype(jnp.bfloat16), dos, (((0,), (0,)), ((), ())),
            preferred_element_type=jnp.float32)


def local_backward(qdoc, kdoc, fused, q_cols, all_kv, head0, keys, values):
    rows = fused.shape[0]
    key_rows, kv_cols = keys.shape
    kv_heads = kv_cols // HEAD_SIZE
    query_group = q_cols // HEAD_SIZE // all_kv
    group_cols = query_group * HEAD_SIZE
    kernel = functools.partial(
        attention_kernel, query_group=query_group, query_blocks=rows // BLK,
        key_offset=key_rows - rows)

    def section(n):
        return pl.BlockSpec((rows, group_cols), lambda g: (0, n * all_kv + head0 + g))

    out_spec = pl.BlockSpec((rows, group_cols), lambda g: (0, g))

    k_spec = pl.BlockSpec((key_rows, HEAD_SIZE), lambda g: (0, g))
    return pl.pallas_call(
        kernel,
        grid=(kv_heads,),
        in_specs=[
            pl.BlockSpec((rows, 1), lambda g: (0, 0)),
            pl.BlockSpec((1, key_rows), lambda g: (0, 0)),
            section(0), section(1), section(2), k_spec, k_spec,
        ],
        out_specs=[out_spec, k_spec, k_spec],
        out_shape=[
            jax.ShapeDtypeStruct((rows, kv_heads * group_cols), jnp.bfloat16),
            jax.ShapeDtypeStruct((key_rows, kv_cols), jnp.float32),
            jax.ShapeDtypeStruct((key_rows, kv_cols), jnp.float32),
        ],
        compiler_params=pltpu.CompilerParams(
            dimension_semantics=("arbitrary",), vmem_limit_bytes=48 * 1024 * 1024,
            allow_input_fusion=[False] * 5 + [True] * 2),
    )(qdoc, kdoc, fused, fused, fused, keys, values)


def per_device(query_matrix, key_matrix, value_matrix, fwd_output, output_gradient, block_docs):
    _, q_all = query_matrix.shape
    kv_all = key_matrix.shape[1]
    peers = lax.axis_size("head")
    q_cols, kv_cols = q_all // peers, kv_all // peers
    sections = (query_matrix, output_gradient, fwd_output, key_matrix, value_matrix)
    outgoing = jnp.concatenate(
        [x[:, p * (x.shape[1] // peers):(p + 1) * (x.shape[1] // peers)]
         for p in range(peers) for x in sections], axis=1)
    fused = lax.all_to_all(outgoing, "head", split_axis=1, concat_axis=0, tiled=True)
    window_extent = fused.shape[0]
    key_part = fused[:, 3 * q_cols:3 * q_cols + kv_cols]
    value_part = fused[:, 3 * q_cols + kv_cols:]
    place = lax.axis_index("ctx")
    blocks_here = window_extent // BLK
    own = REACH * window_extent
    skip = own + BLK - DOC_MOST * BLK

    def docs_of(owner):
        docs = lax.dynamic_slice_in_dim(block_docs, jnp.maximum(owner, 0) * blocks_here, blocks_here, 0)
        return jnp.where(owner >= 0, docs, -1)

    key_docs = jnp.concatenate([docs_of(place - distance) for distance in range(REACH, -1, -1)])
    kdoc = jnp.repeat(key_docs, BLK)[skip:][None, :]
    qdoc = jnp.repeat(docs_of(place), BLK)[:, None]
    all_kv = kv_cols // HEAD_SIZE
    per = kv_cols // CHUNKS
    q_parts, k_parts, v_parts = [], [], []
    for j in range(CHUNKS):
        key_here = key_part[:, j * per:(j + 1) * per]
        value_here = value_part[:, j * per:(j + 1) * per]
        pair = jnp.concatenate([key_here, value_here], axis=1)
        behind = []
        for distance in range(REACH, 0, -1):
            first = max(skip - (REACH - distance) * window_extent, 0)
            if first < window_extent:
                behind.append(shifted(pair[first:], "ctx", distance))
        keys = jnp.concatenate([b[:, :per] for b in behind] + [key_here], axis=0)
        values = jnp.concatenate([b[:, per:] for b in behind] + [value_here], axis=0)

        query_sum, key_partial, value_partial = local_backward(
            qdoc, kdoc, fused, q_cols, all_kv, j * per // HEAD_SIZE, keys, values)

        both = jnp.concatenate([key_partial, value_partial], axis=1)
        total = both[own - skip:]
        for distance in range(1, REACH + 1):
            begin = (REACH - distance) * window_extent
            start = max(begin, skip)
            if start >= begin + window_extent:
                continue
            sent = shifted(
                both[start - skip:begin + window_extent - skip].astype(jnp.bfloat16),
                "ctx", -distance)
            total = total.at[start - begin:].add(sent.astype(jnp.float32))
        q_parts.append(query_sum)
        k_parts.append(total[:, :per].astype(jnp.bfloat16))
        v_parts.append(total[:, per:].astype(jnp.bfloat16))
    finished = jnp.concatenate(q_parts + k_parts + v_parts, axis=1)
    returned = lax.all_to_all(finished, "head", split_axis=0, concat_axis=1, tiled=True)
    width = finished.shape[1]

    def gather(begin, size):
        return jnp.concatenate(
            [returned[:, p * width + begin:p * width + begin + size] for p in range(peers)], axis=1)

    return gather(0, q_cols), gather(q_cols, kv_cols), gather(q_cols + kv_cols, kv_cols)


def solution(mesh):
    return jax.shard_map(
        per_device,
        mesh=mesh,
        in_specs=(
            P(("groups", "ctx", "head"), None),
            P(("groups", "ctx", "head"), None),
            P(("groups", "ctx", "head"), None),
            P(("groups", "ctx", "head"), None),
            P(("groups", "ctx", "head"), None),
            P("groups"),
        ),
        out_specs=(
            P(("groups", "ctx", "head"), None),
            P(("groups", "ctx", "head"), None),
            P(("groups", "ctx", "head"), None),
        ),
        check_vma=False,
    )
```

```python
import functools

import jax
import jax.numpy as jnp
from jax import lax
from jax.experimental import pallas as pl
from jax.experimental.pallas import tpu as pltpu
from jax.sharding import PartitionSpec as P

HEAD_SIZE = 128
BLK = 128
REACH = 2
DOC_MOST = 6
CHUNKS = 2


def shifted(block, axis, distance):
    devices = range(lax.axis_size(axis))
    route = [(i - distance, i) for i in devices if i - distance in devices]
    return lax.ppermute(block, axis, route)


def attention_kernel(qdoc_ref, kdoc_ref, q_ref, do_ref, o_ref, k_ref, v_ref,
                     dq_ref, dk_ref, dv_ref, *, query_group, query_blocks, key_offset):
    scale = HEAD_SIZE ** (-0.5)
    window = DOC_MOST * BLK
    dk_ref[...] = jnp.zeros_like(dk_ref)
    dv_ref[...] = jnp.zeros_like(dv_ref)
    for qb in range(query_blocks):
        rows = pl.ds(qb * BLK, BLK)
        k0 = key_offset + (qb + 1 - DOC_MOST) * BLK
        kwin = k_ref[pl.ds(k0, window), :]
        vwin = v_ref[pl.ds(k0, window), :]
        qs = jnp.concatenate(
            [q_ref[rows, pl.ds(r * HEAD_SIZE, HEAD_SIZE)] for r in range(query_group)], axis=0)
        dos = jnp.concatenate(
            [do_ref[rows, pl.ds(r * HEAD_SIZE, HEAD_SIZE)] for r in range(query_group)], axis=0)
        outs = jnp.concatenate(
            [o_ref[rows, pl.ds(r * HEAD_SIZE, HEAD_SIZE)] for r in range(query_group)], axis=0)
        delta = jnp.sum(dos.astype(jnp.float32) * outs.astype(jnp.float32), axis=1, keepdims=True)
        qd = qdoc_ref[rows, :]
        kd = kdoc_ref[:, pl.ds(k0, window)]
        qpos = lax.broadcasted_iota(jnp.int32, (BLK, window), 0) + (key_offset + qb * BLK)
        kpos = lax.broadcasted_iota(jnp.int32, (BLK, window), 1) + k0
        allowed = (qd == kd) & (kpos <= qpos)
        mask = jnp.concatenate([allowed] * query_group, axis=0)
        scores = scale * lax.dot_general(
            qs, kwin, (((1,), (1,)), ((), ())), preferred_element_type=jnp.float32)
        masked = jnp.where(mask, scores, -1e30)
        top = jnp.max(masked, axis=1, keepdims=True)
        total = jnp.sum(jnp.exp(masked - top), axis=1, keepdims=True)
        lse = top + jnp.log(total)
        probs = jnp.exp(masked - lse)
        dprob = lax.dot_general(
            dos, vwin, (((1,), (1,)), ((), ())), preferred_element_type=jnp.float32)
        dscore = (probs * (dprob - delta)).astype(jnp.bfloat16)
        dq = scale * jnp.dot(dscore, kwin, preferred_element_type=jnp.float32)
        for r in range(query_group):
            dq_ref[rows, pl.ds(r * HEAD_SIZE, HEAD_SIZE)] = (
                dq[r * BLK:(r + 1) * BLK].astype(dq_ref.dtype))
        dk_ref[pl.ds(k0, window), :] += lax.dot_general(
            dscore, qs, (((0,), (0,)), ((), ())), preferred_element_type=jnp.float32)
        dv_ref[pl.ds(k0, window), :] += lax.dot_general(
            probs.astype(jnp.bfloat16), dos, (((0,), (0,)), ((), ())),
            preferred_element_type=jnp.float32)
    dk_ref[...] = scale * dk_ref[...]


def local_backward(qdoc, kdoc, fused, q_cols, all_kv, head0, keys, values):
    rows = fused.shape[0]
    key_rows, kv_cols = keys.shape
    kv_heads = kv_cols // HEAD_SIZE
    query_group = q_cols // HEAD_SIZE // all_kv
    group_cols = query_group * HEAD_SIZE
    kernel = functools.partial(
        attention_kernel, query_group=query_group, query_blocks=rows // BLK,
        key_offset=key_rows - rows)

    def section(n):
        return pl.BlockSpec((rows, group_cols), lambda g: (0, n * all_kv + head0 + g))

    out_spec = pl.BlockSpec((rows, group_cols), lambda g: (0, g))

    k_spec = pl.BlockSpec((key_rows, HEAD_SIZE), lambda g: (0, g))
    return pl.pallas_call(
        kernel,
        grid=(kv_heads,),
        in_specs=[
            pl.BlockSpec((rows, 1), lambda g: (0, 0)),
            pl.BlockSpec((1, key_rows), lambda g: (0, 0)),
            section(0), section(1), section(2), k_spec, k_spec,
        ],
        out_specs=[out_spec, k_spec, k_spec],
        out_shape=[
            jax.ShapeDtypeStruct((rows, kv_heads * group_cols), jnp.bfloat16),
            jax.ShapeDtypeStruct((key_rows, kv_cols), jnp.float32),
            jax.ShapeDtypeStruct((key_rows, kv_cols), jnp.float32),
        ],
        compiler_params=pltpu.CompilerParams(
            dimension_semantics=("arbitrary",), vmem_limit_bytes=48 * 1024 * 1024,
            allow_input_fusion=[True] * 2 + [False] * 3 + [True] * 2),
    )(qdoc, kdoc, fused, fused, fused, keys, values)


def per_device(query_matrix, key_matrix, value_matrix, fwd_output, output_gradient, block_docs):
    _, q_all = query_matrix.shape
    kv_all = key_matrix.shape[1]
    peers = lax.axis_size("head")
    q_cols, kv_cols = q_all // peers, kv_all // peers
    sections = (query_matrix, output_gradient, fwd_output, key_matrix, value_matrix)
    outgoing = jnp.concatenate(
        [x[:, p * (x.shape[1] // peers):(p + 1) * (x.shape[1] // peers)]
         for p in range(peers) for x in sections], axis=1)
    fused = lax.all_to_all(outgoing, "head", split_axis=1, concat_axis=0, tiled=True)
    window_extent = fused.shape[0]
    key_part = fused[:, 3 * q_cols:3 * q_cols + kv_cols]
    value_part = fused[:, 3 * q_cols + kv_cols:]
    place = lax.axis_index("ctx")
    blocks_here = window_extent // BLK
    own = REACH * window_extent
    skip = own + BLK - DOC_MOST * BLK

    def docs_of(owner):
        docs = lax.dynamic_slice_in_dim(block_docs, jnp.maximum(owner, 0) * blocks_here, blocks_here, 0)
        return jnp.where(owner >= 0, docs, -1)

    key_docs = jnp.concatenate([docs_of(place - distance) for distance in range(REACH, -1, -1)])
    kdoc = jnp.repeat(key_docs, BLK)[skip:][None, :]
    qdoc = jnp.repeat(docs_of(place), BLK)[:, None]
    all_kv = kv_cols // HEAD_SIZE
    per = kv_cols // CHUNKS
    q_parts, k_parts, v_parts = [], [], []
    for j in range(CHUNKS):
        key_here = key_part[:, j * per:(j + 1) * per]
        value_here = value_part[:, j * per:(j + 1) * per]
        pair = jnp.concatenate([key_here, value_here], axis=1)
        behind = []
        for distance in range(REACH, 0, -1):
            first = max(skip - (REACH - distance) * window_extent, 0)
            if first < window_extent:
                behind.append(shifted(pair[first:], "ctx", distance))
        keys = jnp.concatenate([b[:, :per] for b in behind] + [key_here], axis=0)
        values = jnp.concatenate([b[:, per:] for b in behind] + [value_here], axis=0)

        query_sum, key_partial, value_partial = local_backward(
            qdoc, kdoc, fused, q_cols, all_kv, j * per // HEAD_SIZE, keys, values)

        both = jnp.concatenate([key_partial, value_partial], axis=1)
        total = both[own - skip:]
        for distance in range(1, REACH + 1):
            begin = (REACH - distance) * window_extent
            start = max(begin, skip)
            if start >= begin + window_extent:
                continue
            sent = shifted(
                both[start - skip:begin + window_extent - skip].astype(jnp.bfloat16),
                "ctx", -distance)
            total = total.at[start - begin:].add(sent.astype(jnp.float32))
        q_parts.append(query_sum)
        k_parts.append(total[:, :per].astype(jnp.bfloat16))
        v_parts.append(total[:, per:].astype(jnp.bfloat16))
    finished = jnp.concatenate(q_parts + k_parts + v_parts, axis=1)
    returned = lax.all_to_all(finished, "head", split_axis=0, concat_axis=1, tiled=True)
    width = finished.shape[1]

    def gather(begin, size):
        return jnp.concatenate(
            [returned[:, p * width + begin:p * width + begin + size] for p in range(peers)], axis=1)

    return gather(0, q_cols), gather(q_cols, kv_cols), gather(q_cols + kv_cols, kv_cols)


def solution(mesh):
    return jax.shard_map(
        per_device,
        mesh=mesh,
        in_specs=(
            P(("groups", "ctx", "head"), None),
            P(("groups", "ctx", "head"), None),
            P(("groups", "ctx", "head"), None),
            P(("groups", "ctx", "head"), None),
            P(("groups", "ctx", "head"), None),
            P("groups"),
        ),
        out_specs=(
            P(("groups", "ctx", "head"), None),
            P(("groups", "ctx", "head"), None),
            P(("groups", "ctx", "head"), None),
        ),
        check_vma=False,
    )
```
